256 devices in a mesh: row: 16 (over y, z_hi, core), col: 16 (over x, z_lo).
Axes of the slice: x: 4, y: 4, z: 8 (z_hi: 2, z_lo: 4; z = z_hi * 4 + z_lo), core: 2. Of those that a mesh axis runs over, the one named last changes fastest.
Arguments:
- features: bfloat16 [32768, 256], P(('row', 'col')), may hold values from -6 to 6
- w_in: bfloat16 [256, 256], replicated, may hold values from -0.375 to 0.375
- bias: float32 [256], replicated, may hold values from -3 to 3
- w_out: bfloat16 [256, 172], replicated, may hold values from -1.5 to 1.5
- tiles: bfloat16 [16, 16, 128, 128, 128], P('row', 'col'), may hold values from 0 to 1.2630181
- tile_rows: int32 [16, 16, 128], P('row', 'col'), may hold values from 0 to 15, as said below
- tile_cols: int32 [16, 16, 128], P('row', 'col'), may hold values from 0 to 15
- tile_count: int32 [16, 16], P('row', 'col'), may hold values from 32 to 128, as said below
- labels: int32 [32768], P(('col', 'row')), may hold values from 0 to 171
Outputs:
- loss: float32 [], replicated
- grad_x: bfloat16 [32768, 256], P(('row', 'col'))
- grad_w_in: float32 [256, 256], replicated
- grad_w_out: float32 [256, 172], replicated
- grad_bias: float32 [256], replicated
The draws below stay inside these ranges and needn't reach their ends.
Inputs may be any that keep to these rules, and one draw needn't show every extreme that they name: `tile_rows`: on each grid entry the pairs of tile row and tile column of all slots are distinct. `tile_count`: some grid entry holds exactly 128 live tiles.
All inputs are finite; a program needn't handle non-finite values.
Results may differ from the reference program's by a relative error of at most 0.0041.
The reference program's roundings to bfloat16 on the way count: a program that leaves them out, or rounds other values in their place, can miss the bound.
Values may be sent and summed in bfloat16 or wider, within the bound.
No kernel may reach another device: no remote copies, remote signals or barrier semaphores. Data moves between devices by JAX's collectives and lax.ppermute only.
A program may use at most 128 MiB of HBM per device.

```python
import math
import jax
import jax.numpy as jnp
from jax import lax

ROWS_DEV = 128
TILE = 128
FEAT = 256
CLASSES = 172
TILE_ROWS = 16
TILE_COLS = 16
MAX_TILES = 128
NODES = 32768
N_ROW = 16
N_COL = 16


def tile_positions(key):
    total = TILE_ROWS * TILE_COLS
    scores = jax.random.randint(jax.random.fold_in(key, 11), (N_ROW, N_COL, total), 0, 1 << 18)
    scores = scores * total + jnp.arange(total, dtype=jnp.int32)
    return jnp.argsort(scores, axis=-1)[..., :MAX_TILES].astype(jnp.int32)


def draw_tile_rows(key, part):
    return tile_positions(key) // TILE_COLS


def draw_tile_cols(key, part):
    return tile_positions(key) % TILE_COLS


def draw_tile_count(key, part):
    counts = jax.random.randint(jax.random.fold_in(key, 21), (N_ROW * N_COL,), MAX_TILES // 4, MAX_TILES + 1)
    chosen = jax.random.randint(jax.random.fold_in(key, 22), (), 0, N_ROW * N_COL)
    counts = jnp.where(jnp.arange(N_ROW * N_COL, dtype=jnp.int32) == chosen, MAX_TILES, counts)
    return counts.reshape(N_ROW, N_COL).astype(jnp.int32)


def draw_tiles(key, part):
    upper = (12.0 / (TILE * TILE_COLS)) ** 0.5
    values = jax.random.uniform(jax.random.fold_in(key, 31), (N_ROW, N_COL, MAX_TILES, TILE, TILE), jnp.float32, 0.0, upper)
    return values.astype(jnp.bfloat16)


def draw_w_out(key, part):
    base = 4.0 / FEAT ** 0.5
    values = jnp.clip(jax.random.normal(jax.random.fold_in(key, 42), (FEAT, CLASSES), jnp.float32), -6.0, 6.0) * base
    return values.astype(jnp.bfloat16)


def set_ends(drawn, own_key, low, high):
    spot = [jax.random.randint(jax.random.fold_in(own_key, axis), (), 0, length) for axis, length in enumerate(drawn.shape)]
    main_axis = drawn.shape.index(max(drawn.shape))
    neighbour = spot[:main_axis] + [(spot[main_axis] + 1) % drawn.shape[main_axis]] + spot[main_axis + 1:]
    return drawn.at[tuple(spot)].set(low).at[tuple(neighbour)].set(high)


def block_scale(own_key, dims, shards, least, largest):
    loudness, own = 1.0, jax.random.fold_in(own_key, 6)
    for position, parts in shards:
        steps = jnp.exp(jax.random.uniform(jax.random.fold_in(own, position), (parts,), jnp.float32, least / len(shards), largest / len(shards)))
        loudness = loudness * jnp.repeat(steps, dims[position] // parts).reshape([-1 if axis == position else 1 for axis in range(len(dims))])
    return loudness


def normal_values(stream_key, dims, scale, reach, split=(), kind=jnp.bfloat16):
    drawn = jax.random.normal(stream_key, dims, jnp.float32) * scale
    if len(split) > 0:
        drawn = block_scale(stream_key, dims, split, -0.22, 0.18) * drawn
    return jnp.clip(drawn, min=-reach, max=reach).astype(kind)


def setup_inputs(seed: int = 0) -> dict:
    splits = jax.random.split(jax.random.key(seed), 10)
    return {
        "features": normal_values(splits[0], (NODES, FEAT), 1.0, 6.0, ((0, 256),)),
        "w_in": normal_values(splits[1], (FEAT, FEAT), FEAT ** -0.5, 0.375),
        "bias": normal_values(splits[2], (FEAT,), 0.5, 3.0, (), jnp.float32),
        "w_out": draw_w_out(jax.random.fold_in(splits[9], 71), 0),
        "tiles": draw_tiles(jax.random.fold_in(splits[9], 71), 0),
        "tile_rows": draw_tile_rows(jax.random.fold_in(splits[9], 71), 0),
        "tile_cols": draw_tile_cols(jax.random.fold_in(splits[9], 71), 0),
        "tile_count": draw_tile_count(jax.random.fold_in(splits[9], 71), 0),
        "labels": set_ends(jax.random.randint(splits[8], (NODES,), 0, CLASSES), jax.random.fold_in(splits[8], 1), 0, CLASSES - 1).astype(jnp.int32),
    }


def forward_tiles(tile_block, row_ids, col_ids, live_count, source, row_count):
    width = source.shape[1]
    pieces = source.reshape(-1, TILE, width)[col_ids]
    products = jnp.einsum('tab,tbf->taf', tile_block.astype(jnp.float32), pieces.astype(jnp.float32))
    live = (jnp.arange(row_ids.shape[0], dtype=jnp.int32) < live_count).astype(jnp.float32)
    products = products * live[:, None, None]
    summed = jnp.zeros((row_count, TILE, width), jnp.float32).at[row_ids].add(products)
    return summed.reshape(row_count * TILE, width)

def backward_tiles(tile_block, row_ids, col_ids, live_count, grads, col_count):
    width = grads.shape[1]
    pieces = grads.reshape(-1, TILE, width)[row_ids]
    products = jnp.einsum('tab,taf->tbf', tile_block.astype(jnp.float32), pieces.astype(jnp.float32))
    live = (jnp.arange(col_ids.shape[0], dtype=jnp.int32) < live_count).astype(jnp.float32)
    products = products * live[:, None, None]
    summed = jnp.zeros((col_count, TILE, width), jnp.float32).at[col_ids].add(products)
    return summed.reshape(col_count * TILE, width)

def reference(features, w_in, bias, w_out, tiles, tile_rows, tile_cols, tile_count, labels):
    row_block = N_ROW * ROWS_DEV
    col_block = N_COL * ROWS_DEV
    proj = jnp.dot(features, w_in, preferred_element_type=jnp.float32).astype(jnp.bfloat16)
    devices = jnp.arange(N_ROW * N_COL, dtype=jnp.int32)

    def forward_step(total, device):
        row_idx = device // N_COL
        col_idx = device % N_COL
        source = lax.dynamic_slice_in_dim(proj, row_idx * col_block, col_block, 0)
        part = forward_tiles(tiles[row_idx, col_idx], tile_rows[row_idx, col_idx], tile_cols[row_idx, col_idx], tile_count[row_idx, col_idx], source, TILE_ROWS)
        current = lax.dynamic_slice_in_dim(total, col_idx * row_block, row_block, 0)
        return (lax.dynamic_update_slice_in_dim(total, current + part, col_idx * row_block, 0), None)
    agg, unused = lax.scan(forward_step, jnp.zeros((NODES, FEAT), jnp.float32), devices)
    pre_act = agg + bias[None, :]
    squash = jax.nn.sigmoid(pre_act)
    hidden = (pre_act * squash).astype(jnp.bfloat16)
    logits = jnp.dot(hidden, w_out, preferred_element_type=jnp.float32)
    top_val = lax.optimization_barrier(jnp.max(logits, axis=1))
    lse = top_val + jnp.log(lax.optimization_barrier(jnp.sum(jnp.exp(logits - top_val[:, None]), axis=1)))
    onehot = (jnp.arange(CLASSES, dtype=jnp.int32)[None, :] == labels[:, None]).astype(jnp.float32)
    picked = lax.optimization_barrier(jnp.sum(logits * onehot, axis=1))
    loss = jnp.sum(lse - picked) / NODES
    dlog = (jnp.exp(logits - lse[:, None]) - onehot).astype(jnp.bfloat16)
    scale = 1.0 / math.sqrt(ROWS_DEV)
    grad_w_out = jnp.dot(hidden.T, dlog, preferred_element_type=jnp.float32) * scale
    d_hidden = jnp.dot(dlog, w_out.T, preferred_element_type=jnp.float32)
    grad_z = (d_hidden * squash * (1.0 + pre_act * (1.0 - squash))).astype(jnp.bfloat16)
    grad_bias = lax.optimization_barrier(jnp.sum(grad_z.astype(jnp.float32), axis=0)) * scale

    def backward_step(total, device):
        row_idx = device // N_COL
        col_idx = device % N_COL
        block = lax.dynamic_slice_in_dim(grad_z, col_idx * row_block, row_block, 0)
        part = backward_tiles(tiles[row_idx, col_idx], tile_rows[row_idx, col_idx], tile_cols[row_idx, col_idx], tile_count[row_idx, col_idx], block, TILE_COLS)
        current = lax.dynamic_slice_in_dim(total, row_idx * col_block, col_block, 0)
        return (lax.dynamic_update_slice_in_dim(total, current + part, row_idx * col_block, 0), None)
    back_total, unused = lax.scan(backward_step, jnp.zeros((NODES, FEAT), jnp.float32), devices)
    grad_proj = back_total.astype(jnp.bfloat16)
    grad_w_in = jnp.dot(features.T, grad_proj, preferred_element_type=jnp.float32) * scale
    grad_x = jnp.dot(grad_proj, w_in.T, preferred_element_type=jnp.float32).astype(jnp.bfloat16)
    return (loss, grad_x, grad_w_in, grad_w_out, grad_bias)
```

```python
import math

import jax
import jax.numpy as jnp
from jax import lax
from jax.experimental import pallas as pl
from jax.experimental.pallas import tpu as pltpu
from jax.sharding import PartitionSpec as P

TILE = 128
CHUNK = 8


def _tile_kernel(transpose, rows_ref, cols_ref, count_ref, tiles_ref, src_ref, out_ref):
    step = pl.program_id(0)
    count = count_ref[0]

    @pl.when(step == 0)
    def _():
        out_ref[...] = jnp.zeros_like(out_ref)

    for j in range(CHUNK):
        slot = step * CHUNK + j

        @pl.when(slot < count)
        def _():
            if transpose:
                src_at = rows_ref[slot]
                dst_at = cols_ref[slot]
            else:
                src_at = cols_ref[slot]
                dst_at = rows_ref[slot]
            src = src_ref[pl.ds(pl.multiple_of(src_at * TILE, TILE), TILE), :]
            tile = tiles_ref[j]
            if transpose:
                part = lax.dot_general(
                    tile, src, (((0,), (0,)), ((), ())), preferred_element_type=jnp.float32
                )
            else:
                part = jnp.dot(tile, src, preferred_element_type=jnp.float32)
            dst = pl.ds(pl.multiple_of(dst_at * TILE, TILE), TILE)
            out_ref[dst, :] += part


def tile_product(tile_block, row_ids, col_ids, live_count, source, out_tiles, transpose):
    slots = tile_block.shape[0]
    width = source.shape[1]
    steps = slots // CHUNK

    def tiles_map(i, rows, cols, count):
        last = jnp.maximum(count[0] - 1, 0) // CHUNK
        return (jnp.minimum(i, last), 0, 0)

    grid_spec = pltpu.PrefetchScalarGridSpec(
        num_scalar_prefetch=3,
        grid=(steps,),
        in_specs=[
            pl.BlockSpec((CHUNK, TILE, TILE), tiles_map),
            pl.BlockSpec(source.shape, lambda i, rows, cols, count: (0, 0)),
        ],
        out_specs=pl.BlockSpec((out_tiles * TILE, width), lambda i, rows, cols, count: (0, 0)),
    )
    return pl.pallas_call(
        lambda *refs: _tile_kernel(transpose, *refs),
        grid_spec=grid_spec,
        out_shape=jax.ShapeDtypeStruct((out_tiles * TILE, width), jnp.float32),
        compiler_params=pltpu.CompilerParams(dimension_semantics=("arbitrary",)),
    )(row_ids, col_ids, live_count.reshape(1), tile_block, source)


def head_block(agg, bias, w_out, node_labels):
    pre_act = agg + bias[None, :]
    squash = jax.nn.sigmoid(pre_act)
    hidden = (pre_act * squash).astype(jnp.bfloat16)
    logits = jnp.dot(hidden, w_out, preferred_element_type=jnp.float32)
    top_val = jnp.max(logits, axis=1)
    lse = top_val + jnp.log(jnp.sum(jnp.exp(logits - top_val[:, None]), axis=1))
    onehot = (jnp.arange(w_out.shape[1], dtype=jnp.int32)[None, :] == node_labels[:, None]).astype(
        jnp.float32
    )
    picked = jnp.sum(logits * onehot, axis=1)
    loss_sum = jnp.sum(lse - picked)
    dlog = (jnp.exp(logits - lse[:, None]) - onehot).astype(jnp.bfloat16)
    out_term = jnp.einsum("nf,nc->fc", hidden, dlog, preferred_element_type=jnp.float32)
    d_hidden = jnp.einsum("nc,fc->nf", dlog, w_out, preferred_element_type=jnp.float32)
    grad_z = (d_hidden * squash * (1.0 + pre_act * (1.0 - squash))).astype(jnp.bfloat16)
    bias_term = jnp.sum(grad_z.astype(jnp.float32), axis=0)
    return (loss_sum, out_term, bias_term, grad_z)


def body(features, w_in, bias, w_out, tiles, tile_rows, tile_cols, tile_count, labels):
    row_devices = lax.axis_size("row")
    col_devices = lax.axis_size("col")
    rows_here = features.shape[0]
    feat = features.shape[1]
    classes = w_out.shape[1]
    nodes = rows_here * row_devices * col_devices
    scale = 1.0 / math.sqrt(rows_here)
    row_tiles = row_devices * rows_here // TILE
    col_tiles = col_devices * rows_here // TILE
    tile_block = tiles[0, 0]
    row_ids = tile_rows[0, 0]
    col_ids = tile_cols[0, 0]
    live_count = tile_count[0, 0]
    proj = jnp.dot(features, w_in, preferred_element_type=jnp.float32).astype(jnp.bfloat16)
    source = lax.all_gather(proj, "col", axis=0, tiled=True)
    partial_value = tile_product(tile_block, row_ids, col_ids, live_count, source, row_tiles, False)
    agg = lax.psum_scatter(partial_value, "row", scatter_dimension=0, tiled=True)
    loss_sum, out_term, bias_term, grad_z = head_block(agg, bias, w_out, labels)
    grad_block = lax.all_gather(grad_z, "row", axis=0, tiled=True)
    back_part = tile_product(tile_block, row_ids, col_ids, live_count, grad_block, col_tiles, True)
    grad_proj = lax.psum_scatter(back_part, "col", scatter_dimension=0, tiled=True).astype(
        jnp.bfloat16
    )
    in_term = jnp.einsum("nf,ng->fg", features, grad_proj, preferred_element_type=jnp.float32)
    extra = jnp.zeros((feat, 2), jnp.float32)
    extra = extra.at[:, 0].set(bias_term).at[0, 1].set(loss_sum)
    packed = jnp.concatenate([in_term, out_term, extra], axis=1)
    packed = lax.psum(packed, ("row", "col"))
    grad_w_in = packed[:, :feat] * scale
    grad_w_out = packed[:, feat : feat + classes] * scale
    grad_bias = packed[:, feat + classes] * scale
    loss = packed[0, feat + classes + 1] / nodes
    grad_x = jnp.einsum("ng,fg->nf", grad_proj, w_in, preferred_element_type=jnp.float32).astype(
        jnp.bfloat16
    )
    return (loss, grad_x, grad_w_in, grad_w_out, grad_bias)


def solution(mesh):
    placed = (
        P(("row", "col"), None),
        P(),
        P(),
        P(),
        P("row", "col", None, None, None),
        P("row", "col", None),
        P("row", "col", None),
        P("row", "col"),
        P(("col", "row")),
    )
    return jax.shard_map(
        body,
        mesh=mesh,
        in_specs=placed,
        out_specs=(P(), P(("row", "col"), None), P(), P(), P()),
        check_vma=False,
    )
```

```python
import math

import jax
import jax.numpy as jnp
from jax import lax
from jax.experimental import pallas as pl
from jax.experimental.pallas import tpu as pltpu
from jax.sharding import PartitionSpec as P

TILE = 128
CHUNK = 8


def _tile_kernel(transpose, rows_ref, cols_ref, count_ref, tiles_ref, src_ref, out_ref):
    step = pl.program_id(0)
    count = count_ref[0]

    @pl.when(step == 0)
    def _():
        out_ref[...] = jnp.zeros_like(out_ref)

    for j in range(CHUNK):
        slot = step * CHUNK + j

        @pl.when(slot < count)
        def _():
            if transpose:
                src_at = rows_ref[slot]
                dst_at = cols_ref[slot]
            else:
                src_at = cols_ref[slot]
                dst_at = rows_ref[slot]
            src = src_ref[pl.ds(pl.multiple_of(src_at * TILE, TILE), TILE), :]
            tile = tiles_ref[j]
            if transpose:
                part = lax.dot_general(
                    tile, src, (((0,), (0,)), ((), ())), preferred_element_type=jnp.float32
                )
            else:
                part = jnp.dot(tile, src, preferred_element_type=jnp.float32)
            dst = pl.ds(pl.multiple_of(dst_at * TILE, TILE), TILE)
            out_ref[dst, :] += part


def tile_product(tile_block, row_ids, col_ids, live_count, source, out_tiles, transpose):
    slots = tile_block.shape[0]
    width = source.shape[1]
    steps = slots // CHUNK

    def tiles_map(i, rows, cols, count):
        last = jnp.maximum(count[0] - 1, 0) // CHUNK
        return (jnp.minimum(i, last), 0, 0)

    grid_spec = pltpu.PrefetchScalarGridSpec(
        num_scalar_prefetch=3,
        grid=(steps,),
        in_specs=[
            pl.BlockSpec((CHUNK, TILE, TILE), tiles_map),
            pl.BlockSpec(source.shape, lambda i, rows, cols, count: (0, 0)),
        ],
        out_specs=pl.BlockSpec((out_tiles * TILE, width), lambda i, rows, cols, count: (0, 0)),
    )
    return pl.pallas_call(
        lambda *refs: _tile_kernel(transpose, *refs),
        grid_spec=grid_spec,
        out_shape=jax.ShapeDtypeStruct((out_tiles * TILE, width), jnp.float32),
        compiler_params=pltpu.CompilerParams(dimension_semantics=("arbitrary",)),
    )(row_ids, col_ids, live_count.reshape(1), tile_block, source)


def gather_rows(x, axis):
    n = lax.axis_size(axis)
    spread = jnp.broadcast_to(x[None], (n,) + x.shape)
    got = lax.all_to_all(spread, axis, 0, 0, tiled=False)
    return got.reshape(n * x.shape[0], x.shape[1])


def scatter_rows(x, axis):
    n = lax.axis_size(axis)
    got = lax.all_to_all(x.reshape(n, -1, x.shape[1]), axis, 0, 0, tiled=False)
    return jnp.sum(got, axis=0)


def reduce_all(x, axes):
    n = lax.psum(1, axes)
    got = lax.all_to_all(x.reshape(n, -1, x.shape[1]), axes, 0, 0, tiled=False)
    mine = jnp.sum(got, axis=0)
    spread = jnp.broadcast_to(mine[None], (n,) + mine.shape)
    back = lax.all_to_all(spread, axes, 0, 0, tiled=False)
    return back.reshape(x.shape)


def head_block(agg, bias, w_out, node_labels):
    pre_act = agg + bias[None, :]
    squash = jax.nn.sigmoid(pre_act)
    hidden = (pre_act * squash).astype(jnp.bfloat16)
    logits = jnp.dot(hidden, w_out, preferred_element_type=jnp.float32)
    top_val = jnp.max(logits, axis=1)
    lse = top_val + jnp.log(jnp.sum(jnp.exp(logits - top_val[:, None]), axis=1))
    onehot = (jnp.arange(w_out.shape[1], dtype=jnp.int32)[None, :] == node_labels[:, None]).astype(
        jnp.float32
    )
    picked = jnp.sum(logits * onehot, axis=1)
    loss_sum = jnp.sum(lse - picked)
    dlog = (jnp.exp(logits - lse[:, None]) - onehot).astype(jnp.bfloat16)
    out_term = jnp.einsum("nf,nc->fc", hidden, dlog, preferred_element_type=jnp.float32)
    d_hidden = jnp.einsum("nc,fc->nf", dlog, w_out, preferred_element_type=jnp.float32)
    grad_z = (d_hidden * squash * (1.0 + pre_act * (1.0 - squash))).astype(jnp.bfloat16)
    bias_term = jnp.sum(grad_z.astype(jnp.float32), axis=0)
    return (loss_sum, out_term, bias_term, grad_z)


def body(features, w_in, bias, w_out, tiles, tile_rows, tile_cols, tile_count, labels):
    row_devices = lax.axis_size("row")
    col_devices = lax.axis_size("col")
    rows_here = features.shape[0]
    feat = features.shape[1]
    classes = w_out.shape[1]
    nodes = rows_here * row_devices * col_devices
    scale = 1.0 / math.sqrt(rows_here)
    row_tiles = row_devices * rows_here // TILE
    col_tiles = col_devices * rows_here // TILE
    tile_block = tiles[0, 0]
    row_ids = tile_rows[0, 0]
    col_ids = tile_cols[0, 0]
    live_count = tile_count[0, 0]
    proj = jnp.dot(features, w_in, preferred_element_type=jnp.float32).astype(jnp.bfloat16)
    source = gather_rows(proj, "col")
    partial_value = tile_product(tile_block, row_ids, col_ids, live_count, source, row_tiles, False)
    agg = scatter_rows(partial_value, "row")
    loss_sum, out_term, bias_term, grad_z = head_block(agg, bias, w_out, labels)
    grad_block = gather_rows(grad_z, "row")
    back_part = tile_product(tile_block, row_ids, col_ids, live_count, grad_block, col_tiles, True)
    grad_proj = scatter_rows(back_part, "col").astype(jnp.bfloat16)
    in_term = jnp.einsum("nf,ng->fg", features, grad_proj, preferred_element_type=jnp.float32)
    extra = jnp.zeros((feat, 2), jnp.float32)
    extra = extra.at[:, 0].set(bias_term).at[0, 1].set(loss_sum)
    packed = jnp.concatenate([in_term, out_term, extra], axis=1)
    packed = reduce_all(packed, ("row", "col"))
    grad_w_in = packed[:, :feat] * scale
    grad_w_out = packed[:, feat : feat + classes] * scale
    grad_bias = packed[:, feat + classes] * scale
    loss = packed[0, feat + classes + 1] / nodes
    grad_x = jnp.einsum("ng,fg->nf", grad_proj, w_in, preferred_element_type=jnp.float32).astype(
        jnp.bfloat16
    )
    return (loss, grad_x, grad_w_in, grad_w_out, grad_bias)


def solution(mesh):
    placed = (
        P(("row", "col"), None),
        P(),
        P(),
        P(),
        P("row", "col", None, None, None),
        P("row", "col", None),
        P("row", "col", None),
        P("row", "col"),
        P(("col", "row")),
    )
    return jax.shard_map(
        body,
        mesh=mesh,
        in_specs=placed,
        out_specs=(P(), P(("row", "col"), None), P(), P(), P()),
        check_vma=False,
    )
```

```python
import math

import jax
import jax.numpy as jnp
from jax import lax
from jax.experimental import pallas as pl
from jax.experimental.pallas import tpu as pltpu
from jax.sharding import Mesh, PartitionSpec as P

TILE = 128
CHUNK = 8


def _tile_kernel(transpose, rows_ref, cols_ref, count_ref, tiles_ref, src_ref, out_ref):
    step = pl.program_id(0)
    count = count_ref[0]

    @pl.when(step == 0)
    def _():
        out_ref[...] = jnp.zeros_like(out_ref)

    for j in range(CHUNK):
        slot = step * CHUNK + j

        @pl.when(slot < count)
        def _():
            if transpose:
                src_at = rows_ref[slot]
                dst_at = cols_ref[slot]
            else:
                src_at = cols_ref[slot]
                dst_at = rows_ref[slot]
            src = src_ref[pl.ds(pl.multiple_of(src_at * TILE, TILE), TILE), :]
            tile = tiles_ref[j]
            if transpose:
                part = lax.dot_general(
                    tile, src, (((0,), (0,)), ((), ())), preferred_element_type=jnp.float32
                )
            else:
                part = jnp.dot(tile, src, preferred_element_type=jnp.float32)
            dst = pl.ds(pl.multiple_of(dst_at * TILE, TILE), TILE)
            out_ref[dst, :] += part


def tile_product(tile_block, row_ids, col_ids, live_count, source, out_tiles, transpose):
    slots = tile_block.shape[0]
    width = source.shape[1]
    steps = slots // CHUNK

    def tiles_map(i, rows, cols, count):
        last = jnp.maximum(count[0] - 1, 0) // CHUNK
        return (jnp.minimum(i, last), 0, 0)

    grid_spec = pltpu.PrefetchScalarGridSpec(
        num_scalar_prefetch=3,
        grid=(steps,),
        in_specs=[
            pl.BlockSpec((CHUNK, TILE, TILE), tiles_map),
            pl.BlockSpec(source.shape, lambda i, rows, cols, count: (0, 0)),
        ],
        out_specs=pl.BlockSpec((out_tiles * TILE, width), lambda i, rows, cols, count: (0, 0)),
    )
    return pl.pallas_call(
        lambda *refs: _tile_kernel(transpose, *refs),
        grid_spec=grid_spec,
        out_shape=jax.ShapeDtypeStruct((out_tiles * TILE, width), jnp.float32),
        compiler_params=pltpu.CompilerParams(dimension_semantics=("arbitrary",)),
    )(row_ids, col_ids, live_count.reshape(1), tile_block, source)


def gather_rows(x, axis):
    n = lax.psum(1, axis)
    spread = jnp.broadcast_to(x[None], (n,) + x.shape)
    got = lax.all_to_all(spread, axis, 0, 0, tiled=False)
    return got.reshape(n * x.shape[0], x.shape[1])


def scatter_rows(x, axis):
    n = lax.psum(1, axis)
    got = lax.all_to_all(x.reshape(n, -1, x.shape[1]), axis, 0, 0, tiled=False)
    return jnp.sum(got, axis=0)


def swap_core(x):
    return lax.ppermute(x, "core", [(0, 1), (1, 0)])


def reduce_all(x, axes):
    half = x.shape[0] // 2
    first = lax.axis_index("core") == 0
    mine = jnp.where(first, x[:half], x[half:])
    other = jnp.where(first, x[half:], x[:half])
    summed = mine + swap_core(other)
    summed = gather_rows(scatter_rows(summed, axes), axes)
    partner = swap_core(summed)
    return jnp.where(first, jnp.concatenate([summed, partner]), jnp.concatenate([partner, summed]))

def head_block(agg, bias, w_out, node_labels):
    pre_act = agg + bias[None, :]
    squash = jax.nn.sigmoid(pre_act)
    hidden = (pre_act * squash).astype(jnp.bfloat16)
    logits = jnp.dot(hidden, w_out, preferred_element_type=jnp.float32)
    top_val = jnp.max(logits, axis=1)
    lse = top_val + jnp.log(jnp.sum(jnp.exp(logits - top_val[:, None]), axis=1))
    onehot = (jnp.arange(w_out.shape[1], dtype=jnp.int32)[None, :] == node_labels[:, None]).astype(
        jnp.float32
    )
    picked = jnp.sum(logits * onehot, axis=1)
    loss_sum = jnp.sum(lse - picked)
    dlog = (jnp.exp(logits - lse[:, None]) - onehot).astype(jnp.bfloat16)
    out_term = jnp.einsum("nf,nc->fc", hidden, dlog, preferred_element_type=jnp.float32)
    d_hidden = jnp.einsum("nc,fc->nf", dlog, w_out, preferred_element_type=jnp.float32)
    grad_z = (d_hidden * squash * (1.0 + pre_act * (1.0 - squash))).astype(jnp.bfloat16)
    bias_term = jnp.sum(grad_z.astype(jnp.float32), axis=0)
    return (loss_sum, out_term, bias_term, grad_z)


def body(features, w_in, bias, w_out, tiles, tile_rows, tile_cols, tile_count, labels):
    row_devices = lax.psum(1, ("rh", "core"))
    col_devices = lax.psum(1, ("cx", "cz"))
    rows_here = features.shape[0]
    feat = features.shape[1]
    classes = w_out.shape[1]
    nodes = rows_here * row_devices * col_devices
    scale = 1.0 / math.sqrt(rows_here)
    row_tiles = row_devices * rows_here // TILE
    col_tiles = col_devices * rows_here // TILE
    tile_block = tiles[0, 0]
    row_ids = tile_rows[0, 0]
    col_ids = tile_cols[0, 0]
    live_count = tile_count[0, 0]
    row_hi = row_ids // 2
    row_pos = jnp.where(row_ids % 2 == lax.axis_index("core"), row_hi, row_hi + row_tiles // 2)
    proj = jnp.dot(features, w_in, preferred_element_type=jnp.float32).astype(jnp.bfloat16)
    source = gather_rows(gather_rows(proj, "cz"), "cx")
    partial_value = tile_product(tile_block, row_pos, col_ids, live_count, source, row_tiles, False)
    half = partial_value.shape[0] // 2
    summed = partial_value[:half] + swap_core(partial_value[half:])
    agg = scatter_rows(summed, "rh")
    loss_sum, out_term, bias_term, grad_z = head_block(agg, bias, w_out, labels)
    gathered = gather_rows(grad_z, "rh")
    grad_block = jnp.concatenate([gathered, swap_core(gathered)])
    back_part = tile_product(tile_block, row_pos, col_ids, live_count, grad_block, col_tiles, True)
    grad_proj = scatter_rows(scatter_rows(back_part, "cx"), "cz").astype(jnp.bfloat16)
    in_term = jnp.einsum("nf,ng->fg", features, grad_proj, preferred_element_type=jnp.float32)
    extra = jnp.zeros((feat, 2), jnp.float32)
    extra = extra.at[:, 0].set(bias_term).at[0, 1].set(loss_sum)
    packed = jnp.concatenate([in_term, out_term, extra], axis=1)
    packed = reduce_all(packed, ("rh", "cx", "cz"))
    grad_w_in = packed[:, :feat] * scale
    grad_w_out = packed[:, feat : feat + classes] * scale
    grad_bias = packed[:, feat + classes] * scale
    loss = packed[0, feat + classes + 1] / nodes
    grad_x = jnp.einsum("ng,fg->nf", grad_proj, w_in, preferred_element_type=jnp.float32).astype(
        jnp.bfloat16
    )
    return (loss, grad_x, grad_w_in, grad_w_out, grad_bias)


def solution(mesh):
    row_size, col_size = mesh.shape["row"], mesh.shape["col"]
    cz = 4 if col_size % 4 == 0 else 1
    fine = Mesh(
        mesh.devices.reshape(row_size // 2, 2, col_size // cz, cz), ("rh", "core", "cx", "cz")
    )
    row, col = ("rh", "core"), ("cx", "cz")
    placed = (
        P(row + col, None),
        P(),
        P(),
        P(),
        P(row, col, None, None, None),
        P(row, col, None),
        P(row, col, None),
        P(row, col),
        P(col + row),
    )
    return jax.shard_map(
        body,
        mesh=fine,
        in_specs=placed,
        out_specs=(P(), P(row + col, None), P(), P(), P()),
        check_vma=False,
    )
```

```python
import math

import jax
import jax.numpy as jnp
from jax import lax
from jax.experimental import pallas as pl
from jax.experimental.pallas import tpu as pltpu
from jax.sharding import Mesh, PartitionSpec as P

TILE = 128
CHUNK = 8


def _dense_kernel(transpose, rows_ref, cols_ref, count_ref, tiles_ref, src_ref, out_ref, dense_ref):
    step = pl.program_id(0)
    count = count_ref[0]

    @pl.when(step == 0)
    def _():
        dense_ref[...] = jnp.zeros_like(dense_ref)

    for j in range(CHUNK):
        slot = step * CHUNK + j

        @pl.when(slot < count)
        def _():
            at_row = pl.multiple_of(rows_ref[slot] * TILE, TILE)
            at_col = pl.multiple_of(cols_ref[slot] * TILE, TILE)
            dense_ref[pl.ds(at_row, TILE), pl.ds(at_col, TILE)] = tiles_ref[j]

    @pl.when(step == pl.num_programs(0) - 1)
    def _():
        if transpose:
            out_ref[...] = jnp.dot(src_ref[...], dense_ref[...], preferred_element_type=jnp.float32)
        else:
            out_ref[...] = jnp.dot(dense_ref[...], src_ref[...], preferred_element_type=jnp.float32)


def tile_product(tile_block, row_ids, col_ids, live_count, source, out_tiles, transpose):
    slots = tile_block.shape[0]
    width = source.shape[1]
    steps = slots // CHUNK
    src_tiles = source.shape[0] // TILE
    dense_shape = (out_tiles * TILE, src_tiles * TILE)
    if transpose:
        source = source.T
        dense_shape = (src_tiles * TILE, out_tiles * TILE)
        out_shape = (width, out_tiles * TILE)
    else:
        out_shape = (out_tiles * TILE, width)

    def tiles_map(i, rows, cols, count):
        last = jnp.maximum(count[0] - 1, 0) // CHUNK
        return (jnp.minimum(i, last), 0, 0)

    grid_spec = pltpu.PrefetchScalarGridSpec(
        num_scalar_prefetch=3,
        grid=(steps,),
        in_specs=[
            pl.BlockSpec((CHUNK, TILE, TILE), tiles_map),
            pl.BlockSpec(source.shape, lambda i, rows, cols, count: (0, 0)),
        ],
        out_specs=pl.BlockSpec(out_shape, lambda i, rows, cols, count: (0, 0)),
        scratch_shapes=[pltpu.VMEM(dense_shape, jnp.bfloat16)],
    )
    result = pl.pallas_call(
        lambda *refs: _dense_kernel(transpose, *refs),
        grid_spec=grid_spec,
        out_shape=jax.ShapeDtypeStruct(out_shape, jnp.float32),
        compiler_params=pltpu.CompilerParams(dimension_semantics=("arbitrary",)),
    )(row_ids, col_ids, live_count.reshape(1), tile_block, source)
    return result.T if transpose else result


def gather_rows(x, axis):
    n = lax.psum(1, axis)
    spread = jnp.broadcast_to(x[None], (n,) + x.shape)
    got = lax.all_to_all(spread, axis, 0, 0, tiled=False)
    return got.reshape(n * x.shape[0], x.shape[1])


def scatter_rows(x, axis):
    n = lax.psum(1, axis)
    got = lax.all_to_all(x.reshape(n, -1, x.shape[1]), axis, 0, 0, tiled=False)
    return jnp.sum(got, axis=0)


def swap_core(x):
    return lax.ppermute(x, "core", [(0, 1), (1, 0)])


def reduce_all(x, axes):
    half = x.shape[0] // 2
    first = lax.axis_index("core") == 0
    mine = jnp.where(first, x[:half], x[half:])
    other = jnp.where(first, x[half:], x[:half])
    summed = mine + swap_core(other)
    summed = gather_rows(scatter_rows(summed, axes), axes)
    partner = swap_core(summed)
    return jnp.where(first, jnp.concatenate([summed, partner]), jnp.concatenate([partner, summed]))

def head_block(agg, bias, w_out, node_labels):
    pre_act = agg + bias[None, :]
    squash = jax.nn.sigmoid(pre_act)
    hidden = (pre_act * squash).astype(jnp.bfloat16)
    logits = jnp.dot(hidden, w_out, preferred_element_type=jnp.float32)
    top_val = jnp.max(logits, axis=1)
    lse = top_val + jnp.log(jnp.sum(jnp.exp(logits - top_val[:, None]), axis=1))
    onehot = (jnp.arange(w_out.shape[1], dtype=jnp.int32)[None, :] == node_labels[:, None]).astype(
        jnp.float32
    )
    picked = jnp.sum(logits * onehot, axis=1)
    loss_sum = jnp.sum(lse - picked)
    dlog = (jnp.exp(logits - lse[:, None]) - onehot).astype(jnp.bfloat16)
    out_term = jnp.einsum("nf,nc->fc", hidden, dlog, preferred_element_type=jnp.float32)
    d_hidden = jnp.einsum("nc,fc->nf", dlog, w_out, preferred_element_type=jnp.float32)
    grad_z = (d_hidden * squash * (1.0 + pre_act * (1.0 - squash))).astype(jnp.bfloat16)
    bias_term = jnp.sum(grad_z.astype(jnp.float32), axis=0)
    return (loss_sum, out_term, bias_term, grad_z)


def body(features, w_in, bias, w_out, tiles, tile_rows, tile_cols, tile_count, labels):
    row_devices = lax.psum(1, ("rh", "core"))
    col_devices = lax.psum(1, ("cx", "cz"))
    rows_here = features.shape[0]
    feat = features.shape[1]
    classes = w_out.shape[1]
    nodes = rows_here * row_devices * col_devices
    scale = 1.0 / math.sqrt(rows_here)
    row_tiles = row_devices * rows_here // TILE
    col_tiles = col_devices * rows_here // TILE
    tile_block = tiles[0, 0]
    row_ids = tile_rows[0, 0]
    col_ids = tile_cols[0, 0]
    live_count = tile_count[0, 0]
    row_hi = row_ids // 2
    row_pos = jnp.where(row_ids % 2 == lax.axis_index("core"), row_hi, row_hi + row_tiles // 2)
    proj = jnp.dot(features, w_in, preferred_element_type=jnp.float32).astype(jnp.bfloat16)
    source = gather_rows(gather_rows(proj, "cz"), "cx")
    partial_value = tile_product(tile_block, row_pos, col_ids, live_count, source, row_tiles, False)
    half = partial_value.shape[0] // 2
    summed = partial_value[:half] + swap_core(partial_value[half:])
    agg = scatter_rows(summed, "rh")
    loss_sum, out_term, bias_term, grad_z = head_block(agg, bias, w_out, labels)
    gathered = gather_rows(grad_z, "rh")
    grad_block = jnp.concatenate([gathered, swap_core(gathered)])
    back_part = tile_product(tile_block, row_pos, col_ids, live_count, grad_block, col_tiles, True)
    grad_proj = scatter_rows(scatter_rows(back_part, "cx"), "cz").astype(jnp.bfloat16)
    in_term = jnp.einsum("nf,ng->fg", features, grad_proj, preferred_element_type=jnp.float32)
    extra = jnp.zeros((feat, 2), jnp.float32)
    extra = extra.at[:, 0].set(bias_term).at[0, 1].set(loss_sum)
    packed = jnp.concatenate([in_term, out_term, extra], axis=1)
    packed = reduce_all(packed, ("rh", "cx", "cz"))
    grad_w_in = packed[:, :feat] * scale
    grad_w_out = packed[:, feat : feat + classes] * scale
    grad_bias = packed[:, feat + classes] * scale
    loss = packed[0, feat + classes + 1] / nodes
    grad_x = jnp.einsum("ng,fg->nf", grad_proj, w_in, preferred_element_type=jnp.float32).astype(
        jnp.bfloat16
    )
    return (loss, grad_x, grad_w_in, grad_w_out, grad_bias)


def solution(mesh):
    row_size, col_size = mesh.shape["row"], mesh.shape["col"]
    cz = 4 if col_size % 4 == 0 else 1
    fine = Mesh(
        mesh.devices.reshape(row_size // 2, 2, col_size // cz, cz), ("rh", "core", "cx", "cz")
    )
    row, col = ("rh", "core"), ("cx", "cz")
    placed = (
        P(row + col, None),
        P(),
        P(),
        P(),
        P(row, col, None, None, None),
        P(row, col, None),
        P(row, col, None),
        P(row, col),
        P(col + row),
    )
    return jax.shard_map(
        body,
        mesh=fine,
        in_specs=placed,
        out_specs=(P(), P(row + col, None), P(), P(), P()),
        check_vma=False,
    )
```

```python
import math

import jax
import jax.numpy as jnp
from jax import lax
from jax.experimental import pallas as pl
from jax.experimental.pallas import tpu as pltpu
from jax.sharding import Mesh, PartitionSpec as P

TILE = 128
CHUNK = 8


def _dense_kernel(transpose, rows_ref, cols_ref, count_ref, tiles_ref, src_ref, out_ref, dense_ref):
    step = pl.program_id(0)
    count = count_ref[0]

    @pl.when(step == 0)
    def _():
        dense_ref[...] = jnp.zeros_like(dense_ref)

    for j in range(CHUNK):
        slot = step * CHUNK + j

        @pl.when(slot < count)
        def _():
            at_row = pl.multiple_of(rows_ref[slot] * TILE, TILE)
            at_col = pl.multiple_of(cols_ref[slot] * TILE, TILE)
            dense_ref[pl.ds(at_row, TILE), pl.ds(at_col, TILE)] = tiles_ref[j]

    @pl.when(step == pl.num_programs(0) - 1)
    def _():
        if transpose:
            out_ref[...] = jnp.dot(src_ref[...], dense_ref[...], preferred_element_type=jnp.float32)
        else:
            out_ref[...] = jnp.dot(dense_ref[...], src_ref[...], preferred_element_type=jnp.float32)


def tile_product(tile_block, row_ids, col_ids, live_count, source, out_tiles, transpose):
    slots = tile_block.shape[0]
    width = source.shape[1]
    steps = slots // CHUNK
    src_tiles = source.shape[0] // TILE
    dense_shape = (out_tiles * TILE, src_tiles * TILE)
    if transpose:
        source = source.T
        dense_shape = (src_tiles * TILE, out_tiles * TILE)
        out_shape = (width, out_tiles * TILE)
    else:
        out_shape = (out_tiles * TILE, width)

    def tiles_map(i, rows, cols, count):
        last = jnp.maximum(count[0] - 1, 0) // CHUNK
        return (jnp.minimum(i, last), 0, 0)

    grid_spec = pltpu.PrefetchScalarGridSpec(
        num_scalar_prefetch=3,
        grid=(steps,),
        in_specs=[
            pl.BlockSpec((CHUNK, TILE, TILE), tiles_map),
            pl.BlockSpec(source.shape, lambda i, rows, cols, count: (0, 0)),
        ],
        out_specs=pl.BlockSpec(out_shape, lambda i, rows, cols, count: (0, 0)),
        scratch_shapes=[pltpu.VMEM(dense_shape, jnp.bfloat16)],
    )
    result = pl.pallas_call(
        lambda *refs: _dense_kernel(transpose, *refs),
        grid_spec=grid_spec,
        out_shape=jax.ShapeDtypeStruct(out_shape, jnp.float32),
        compiler_params=pltpu.CompilerParams(dimension_semantics=("arbitrary",)),
    )(row_ids, col_ids, live_count.reshape(1), tile_block, source)
    return result.T if transpose else result


def gather_rows(x, axis):
    n = lax.psum(1, axis)
    spread = jnp.broadcast_to(x[None], (n,) + x.shape)
    got = lax.all_to_all(spread, axis, 0, 0, tiled=False)
    return got.reshape(n * x.shape[0], x.shape[1])


def scatter_rows(x, axis):
    n = lax.psum(1, axis)
    got = lax.all_to_all(x.reshape(n, -1, x.shape[1]), axis, 0, 0, tiled=False)
    return jnp.sum(got, axis=0)


def swap_core(x):
    return lax.ppermute(x, "core", [(0, 1), (1, 0)])


def reduce_all(x, axes):
    half = x.shape[0] // 2
    first = lax.axis_index("core") == 0
    mine = jnp.where(first, x[:half], x[half:])
    other = jnp.where(first, x[half:], x[:half])
    summed = mine + swap_core(other)
    summed = gather_rows(scatter_rows(summed, axes), axes)
    partner = swap_core(summed)
    return jnp.where(first, jnp.concatenate([summed, partner]), jnp.concatenate([partner, summed]))

def head_block(agg, bias, w_out, node_labels):
    pre_act = agg + bias[None, :]
    squash = jax.nn.sigmoid(pre_act)
    hidden = (pre_act * squash).astype(jnp.bfloat16)
    logits = jnp.dot(hidden, w_out, preferred_element_type=jnp.float32)
    top_val = jnp.max(logits, axis=1)
    lse = top_val + jnp.log(jnp.sum(jnp.exp(logits - top_val[:, None]), axis=1))
    onehot = (jnp.arange(w_out.shape[1], dtype=jnp.int32)[None, :] == node_labels[:, None]).astype(
        jnp.float32
    )
    picked = jnp.sum(logits * onehot, axis=1)
    loss_sum = jnp.sum(lse - picked)
    dlog = (jnp.exp(logits - lse[:, None]) - onehot).astype(jnp.bfloat16)
    out_term = jnp.einsum("nf,nc->fc", hidden, dlog, preferred_element_type=jnp.float32)
    d_hidden = jnp.einsum("nc,fc->nf", dlog, w_out, preferred_element_type=jnp.float32)
    grad_z = (d_hidden * squash * (1.0 + pre_act * (1.0 - squash))).astype(jnp.bfloat16)
    bias_term = jnp.sum(grad_z.astype(jnp.float32), axis=0)
    return (loss_sum, out_term, bias_term, grad_z)


def body(features, w_in, bias, w_out, tiles, tile_rows, tile_cols, tile_count, labels):
    row_devices = lax.psum(1, ("y", "zh", "core"))
    col_devices = lax.psum(1, ("cx", "cz"))
    rows_here = features.shape[0]
    feat = features.shape[1]
    classes = w_out.shape[1]
    nodes = rows_here * row_devices * col_devices
    scale = 1.0 / math.sqrt(rows_here)
    row_tiles = row_devices * rows_here // TILE
    col_tiles = col_devices * rows_here // TILE
    tile_block = tiles[0, 0]
    row_ids = tile_rows[0, 0]
    col_ids = tile_cols[0, 0]
    live_count = tile_count[0, 0]
    row_hi = row_ids // 2
    row_pos = jnp.where(row_ids % 2 == lax.axis_index("core"), row_hi, row_hi + row_tiles // 2)
    proj = jnp.dot(features, w_in, preferred_element_type=jnp.float32).astype(jnp.bfloat16)
    source = gather_rows(gather_rows(proj, "cz"), "cx")
    partial_value = tile_product(tile_block, row_pos, col_ids, live_count, source, row_tiles, False)
    half = partial_value.shape[0] // 2
    summed = partial_value[:half] + swap_core(partial_value[half:])
    agg = scatter_rows(scatter_rows(summed, "y"), "zh")
    loss_sum, out_term, bias_term, grad_z = head_block(agg, bias, w_out, labels)
    gathered = gather_rows(grad_z, ("y", "zh"))
    grad_block = jnp.concatenate([gathered, swap_core(gathered)])
    back_part = tile_product(tile_block, row_pos, col_ids, live_count, grad_block, col_tiles, True)
    grad_proj = scatter_rows(scatter_rows(back_part, "cx"), "cz").astype(jnp.bfloat16)
    in_term = jnp.einsum("nf,ng->fg", features, grad_proj, preferred_element_type=jnp.float32)
    extra = jnp.zeros((feat, 2), jnp.float32)
    extra = extra.at[:, 0].set(bias_term).at[0, 1].set(loss_sum)
    packed = jnp.concatenate([in_term, out_term, extra], axis=1)
    packed = reduce_all(packed, ("y", "zh", "cx", "cz"))
    grad_w_in = packed[:, :feat] * scale
    grad_w_out = packed[:, feat : feat + classes] * scale
    grad_bias = packed[:, feat + classes] * scale
    loss = packed[0, feat + classes + 1] / nodes
    grad_x = jnp.einsum("ng,fg->nf", grad_proj, w_in, preferred_element_type=jnp.float32).astype(
        jnp.bfloat16
    )
    return (loss, grad_x, grad_w_in, grad_w_out, grad_bias)


def solution(mesh):
    row_size, col_size = mesh.shape["row"], mesh.shape["col"]
    cz = 4 if col_size % 4 == 0 else 1
    fine = Mesh(
        mesh.devices.reshape(row_size // 4, 2, 2, col_size // cz, cz),
        ("y", "zh", "core", "cx", "cz"),
    )
    row, col = ("y", "zh", "core"), ("cx", "cz")
    placed = (
        P(row + col, None),
        P(),
        P(),
        P(),
        P(row, col, None, None, None),
        P(row, col, None),
        P(row, col, None),
        P(row, col),
        P(col + row),
    )
    return jax.shard_map(
        body,
        mesh=fine,
        in_specs=placed,
        out_specs=(P(), P(row + col, None), P(), P(), P()),
        check_vma=False,
    )
```

```python
import math

import jax
import jax.numpy as jnp
from jax import lax
from jax.experimental import pallas as pl
from jax.experimental.pallas import tpu as pltpu
from jax.sharding import Mesh, PartitionSpec as P

TILE = 128
CHUNK = 8


def _dense_kernel(transpose, rows_ref, cols_ref, count_ref, tiles_ref, src_ref, out_ref, dense_ref):
    step = pl.program_id(0)
    count = count_ref[0]

    @pl.when(step == 0)
    def _():
        dense_ref[...] = jnp.zeros_like(dense_ref)

    for j in range(CHUNK):
        slot = step * CHUNK + j

        @pl.when(slot < count)
        def _():
            at_row = pl.multiple_of(rows_ref[slot] * TILE, TILE)
            at_col = pl.multiple_of(cols_ref[slot] * TILE, TILE)
            dense_ref[pl.ds(at_row, TILE), pl.ds(at_col, TILE)] = tiles_ref[j]

    @pl.when(step == pl.num_programs(0) - 1)
    def _():
        if transpose:
            out_ref[...] = jnp.dot(src_ref[...], dense_ref[...], preferred_element_type=jnp.float32)
        else:
            out_ref[...] = jnp.dot(dense_ref[...], src_ref[...], preferred_element_type=jnp.float32)


def tile_product(tile_block, row_ids, col_ids, live_count, source, out_tiles, transpose):
    slots = tile_block.shape[0]
    width = source.shape[1]
    steps = slots // CHUNK
    src_tiles = source.shape[0] // TILE
    dense_shape = (out_tiles * TILE, src_tiles * TILE)
    if transpose:
        source = source.T
        dense_shape = (src_tiles * TILE, out_tiles * TILE)
        out_shape = (width, out_tiles * TILE)
    else:
        out_shape = (out_tiles * TILE, width)

    def tiles_map(i, rows, cols, count):
        last = jnp.maximum(count[0] - 1, 0) // CHUNK
        return (jnp.minimum(i, last), 0, 0)

    grid_spec = pltpu.PrefetchScalarGridSpec(
        num_scalar_prefetch=3,
        grid=(steps,),
        in_specs=[
            pl.BlockSpec((CHUNK, TILE, TILE), tiles_map),
            pl.BlockSpec(source.shape, lambda i, rows, cols, count: (0, 0)),
        ],
        out_specs=pl.BlockSpec(out_shape, lambda i, rows, cols, count: (0, 0)),
        scratch_shapes=[pltpu.VMEM(dense_shape, jnp.bfloat16)],
    )
    result = pl.pallas_call(
        lambda *refs: _dense_kernel(transpose, *refs),
        grid_spec=grid_spec,
        out_shape=jax.ShapeDtypeStruct(out_shape, jnp.float32),
        compiler_params=pltpu.CompilerParams(dimension_semantics=("arbitrary",)),
    )(row_ids, col_ids, live_count.reshape(1), tile_block, source)
    return result.T if transpose else result


def gather_rows(x, axis):
    n = lax.psum(1, axis)
    spread = jnp.broadcast_to(x[None], (n,) + x.shape)
    got = lax.all_to_all(spread, axis, 0, 0, tiled=False)
    return got.reshape(n * x.shape[0], x.shape[1])


def scatter_rows(x, axis, kind=None):
    n = lax.psum(1, axis)
    sent = x.reshape(n, -1, x.shape[1])
    if kind is not None:
        sent = sent.astype(kind)
    got = lax.all_to_all(sent, axis, 0, 0, tiled=False)
    return jnp.sum(got.astype(jnp.float32), axis=0)


def swap_core(x):
    return lax.ppermute(x, "core", [(0, 1), (1, 0)])


def reduce_all(x, axes):
    half = x.shape[0] // 2
    first = lax.axis_index("core") == 0
    mine = jnp.where(first, x[:half], x[half:])
    other = jnp.where(first, x[half:], x[:half])
    summed = mine + swap_core(other)
    summed = gather_rows(scatter_rows(summed, axes), axes)
    partner = swap_core(summed)
    return jnp.where(first, jnp.concatenate([summed, partner]), jnp.concatenate([partner, summed]))

def head_block(agg, bias, w_out, node_labels):
    pre_act = agg + bias[None, :]
    squash = jax.nn.sigmoid(pre_act)
    hidden = (pre_act * squash).astype(jnp.bfloat16)
    logits = jnp.dot(hidden, w_out, preferred_element_type=jnp.float32)
    top_val = jnp.max(logits, axis=1)
    lse = top_val + jnp.log(jnp.sum(jnp.exp(logits - top_val[:, None]), axis=1))
    onehot = (jnp.arange(w_out.shape[1], dtype=jnp.int32)[None, :] == node_labels[:, None]).astype(
        jnp.float32
    )
    picked = jnp.sum(logits * onehot, axis=1)
    loss_sum = jnp.sum(lse - picked)
    dlog = (jnp.exp(logits - lse[:, None]) - onehot).astype(jnp.bfloat16)
    out_term = jnp.einsum("nf,nc->fc", hidden, dlog, preferred_element_type=jnp.float32)
    d_hidden = jnp.einsum("nc,fc->nf", dlog, w_out, preferred_element_type=jnp.float32)
    grad_z = (d_hidden * squash * (1.0 + pre_act * (1.0 - squash))).astype(jnp.bfloat16)
    bias_term = jnp.sum(grad_z.astype(jnp.float32), axis=0)
    return (loss_sum, out_term, bias_term, grad_z)


def body(features, w_in, bias, w_out, tiles, tile_rows, tile_cols, tile_count, labels):
    row_devices = lax.psum(1, ("y", "zh", "core"))
    col_devices = lax.psum(1, ("cx", "cz"))
    rows_here = features.shape[0]
    feat = features.shape[1]
    classes = w_out.shape[1]
    nodes = rows_here * row_devices * col_devices
    scale = 1.0 / math.sqrt(rows_here)
    row_tiles = row_devices * rows_here // TILE
    col_tiles = col_devices * rows_here // TILE
    tile_block = tiles[0, 0]
    row_ids = tile_rows[0, 0]
    col_ids = tile_cols[0, 0]
    live_count = tile_count[0, 0]
    row_hi = row_ids // 2
    row_pos = jnp.where(row_ids % 2 == lax.axis_index("core"), row_hi, row_hi + row_tiles // 2)
    proj = jnp.dot(features, w_in, preferred_element_type=jnp.float32).astype(jnp.bfloat16)
    source = gather_rows(gather_rows(proj, "cz"), "cx")
    partial_value = tile_product(tile_block, row_pos, col_ids, live_count, source, row_tiles, False)
    half = partial_value.shape[0] // 2
    summed = partial_value[:half] + swap_core(partial_value[half:])
    agg = scatter_rows(scatter_rows(summed, "y", jnp.bfloat16), "zh")
    loss_sum, out_term, bias_term, grad_z = head_block(agg, bias, w_out, labels)
    gathered = gather_rows(grad_z, ("y", "zh"))
    grad_block = jnp.concatenate([gathered, swap_core(gathered)])
    back_part = tile_product(tile_block, row_pos, col_ids, live_count, grad_block, col_tiles, True)
    grad_proj = scatter_rows(scatter_rows(back_part, "cx", jnp.bfloat16), "cz").astype(jnp.bfloat16)
    in_term = jnp.einsum("nf,ng->fg", features, grad_proj, preferred_element_type=jnp.float32)
    extra = jnp.zeros((feat, 2), jnp.float32)
    extra = extra.at[:, 0].set(bias_term).at[0, 1].set(loss_sum)
    packed = jnp.concatenate([in_term, out_term, extra], axis=1)
    packed = reduce_all(packed, ("y", "zh", "cx", "cz"))
    grad_w_in = packed[:, :feat] * scale
    grad_w_out = packed[:, feat : feat + classes] * scale
    grad_bias = packed[:, feat + classes] * scale
    loss = packed[0, feat + classes + 1] / nodes
    grad_x = jnp.einsum("ng,fg->nf", grad_proj, w_in, preferred_element_type=jnp.float32).astype(
        jnp.bfloat16
    )
    return (loss, grad_x, grad_w_in, grad_w_out, grad_bias)


def solution(mesh):
    row_size, col_size = mesh.shape["row"], mesh.shape["col"]
    cz = 4 if col_size % 4 == 0 else 1
    fine = Mesh(
        mesh.devices.reshape(row_size // 4, 2, 2, col_size // cz, cz),
        ("y", "zh", "core", "cx", "cz"),
    )
    row, col = ("y", "zh", "core"), ("cx", "cz")
    placed = (
        P(row + col, None),
        P(),
        P(),
        P(),
        P(row, col, None, None, None),
        P(row, col, None),
        P(row, col, None),
        P(row, col),
        P(col + row),
    )
    return jax.shard_map(
        body,
        mesh=fine,
        in_specs=placed,
        out_specs=(P(), P(row + col, None), P(), P(), P()),
        check_vma=False,
    )
```

```python
import math

import jax
import jax.numpy as jnp
from jax import lax
from jax.experimental import pallas as pl
from jax.experimental.pallas import tpu as pltpu
from jax.sharding import Mesh, PartitionSpec as P

TILE = 128
CHUNK = 32


def _dense_kernel(transpose, rows_ref, cols_ref, count_ref, tiles_ref, src_a, src_b, out_a, out_b, dense_ref):
    step = pl.program_id(0)
    count = count_ref[0]

    @pl.when(step == 0)
    def _():
        dense_ref[...] = jnp.zeros_like(dense_ref)

    for j in range(CHUNK):
        slot = step * CHUNK + j

        @pl.when(slot < count)
        def _():
            at_row = pl.multiple_of(rows_ref[slot] * TILE, TILE)
            at_col = pl.multiple_of(cols_ref[slot] * TILE, TILE)
            dense_ref[pl.ds(at_row, TILE), pl.ds(at_col, TILE)] = tiles_ref[j]

    @pl.when(step == pl.num_programs(0) - 1)
    def _():
        half = dense_ref.shape[0] // 2
        if transpose:
            dims = (((0,), (0,)), ((), ()))
            res = lax.dot_general(src_a[...], dense_ref[:half, :], dims, preferred_element_type=jnp.float32)
            res += lax.dot_general(src_b[...], dense_ref[half:, :], dims, preferred_element_type=jnp.float32)
            out_a[...] = res
        else:
            src = src_a[...]
            out_a[...] = jnp.dot(dense_ref[:half, :], src, preferred_element_type=jnp.float32)
            out_b[...] = jnp.dot(dense_ref[half:, :], src, preferred_element_type=jnp.float32)


def tile_product(tile_block, row_ids, col_ids, live_count, sources, out_tiles, transpose):
    slots = tile_block.shape[0]
    width = sources[0].shape[1]
    steps = slots // CHUNK
    if transpose:
        src_tiles = 2 * sources[0].shape[0] // TILE
        dense_shape = (src_tiles * TILE, out_tiles * TILE)
        out_shapes = [(width, out_tiles * TILE), (8, 128)]
    else:
        sources = (sources[0], jnp.zeros((8, 128), sources[0].dtype))
        src_tiles = sources[0].shape[0] // TILE
        dense_shape = (out_tiles * TILE, src_tiles * TILE)
        out_shapes = [(out_tiles * TILE // 2, width)] * 2

    def tiles_map(i, rows, cols, count):
        last = jnp.maximum(count[0] - 1, 0) // CHUNK
        return (jnp.minimum(i, last), 0, 0)

    def whole(shape):
        return pl.BlockSpec(shape, lambda i, rows, cols, count: (0, 0))

    grid_spec = pltpu.PrefetchScalarGridSpec(
        num_scalar_prefetch=3,
        grid=(steps,),
        in_specs=[pl.BlockSpec((CHUNK, TILE, TILE), tiles_map)] + [whole(x.shape) for x in sources],
        out_specs=[whole(shape) for shape in out_shapes],
        scratch_shapes=[pltpu.VMEM(dense_shape, jnp.bfloat16)],
    )
    first, second = pl.pallas_call(
        lambda *refs: _dense_kernel(transpose, *refs),
        grid_spec=grid_spec,
        out_shape=[jax.ShapeDtypeStruct(shape, jnp.float32) for shape in out_shapes],
        compiler_params=pltpu.CompilerParams(dimension_semantics=("arbitrary",)),
    )(row_ids, col_ids, live_count.reshape(1), tile_block, *sources)
    if transpose:
        return first.T
    return first, second


def gather_rows(x, axis):
    n = lax.psum(1, axis)
    spread = jnp.broadcast_to(x[None], (n,) + x.shape)
    got = lax.all_to_all(spread, axis, 0, 0, tiled=False)
    return got.reshape(n * x.shape[0], x.shape[1])


def scatter_rows(x, axis):
    n = lax.psum(1, axis)
    got = lax.all_to_all(x.reshape(n, -1, x.shape[1]), axis, 0, 0, tiled=False)
    return jnp.sum(got, axis=0)


def swap_core(x):
    return lax.ppermute(x, "core", [(0, 1), (1, 0)])


def reduce_all(x, axes):
    half = x.shape[0] // 2
    first = lax.axis_index("core") == 0
    mine = jnp.where(first, x[:half], x[half:])
    other = jnp.where(first, x[half:], x[:half])
    summed = mine + swap_core(other)
    summed = gather_rows(scatter_rows(summed, axes), axes)
    partner = swap_core(summed)
    return jnp.where(first, jnp.concatenate([summed, partner]), jnp.concatenate([partner, summed]))

def head_block(agg, bias, w_out, node_labels):
    pre_act = agg + bias[None, :]
    squash = jax.nn.sigmoid(pre_act)
    hidden = (pre_act * squash).astype(jnp.bfloat16)
    logits = jnp.dot(hidden, w_out, preferred_element_type=jnp.float32)
    top_val = jnp.max(logits, axis=1)
    lse = top_val + jnp.log(jnp.sum(jnp.exp(logits - top_val[:, None]), axis=1))
    onehot = (jnp.arange(w_out.shape[1], dtype=jnp.int32)[None, :] == node_labels[:, None]).astype(
        jnp.float32
    )
    picked = jnp.sum(logits * onehot, axis=1)
    loss_sum = jnp.sum(lse - picked)
    dlog = (jnp.exp(logits - lse[:, None]) - onehot).astype(jnp.bfloat16)
    out_term = jnp.einsum("nf,nc->fc", hidden, dlog, preferred_element_type=jnp.float32)
    d_hidden = jnp.einsum("nc,fc->nf", dlog, w_out, preferred_element_type=jnp.float32)
    grad_z = (d_hidden * squash * (1.0 + pre_act * (1.0 - squash))).astype(jnp.bfloat16)
    bias_term = jnp.sum(grad_z.astype(jnp.float32), axis=0)
    return (loss_sum, out_term, bias_term, grad_z)


def body(features, w_in, bias, w_out, tiles, tile_rows, tile_cols, tile_count, labels):
    row_devices = lax.psum(1, ("y", "zh", "core"))
    col_devices = lax.psum(1, ("cx", "cz"))
    rows_here = features.shape[0]
    feat = features.shape[1]
    classes = w_out.shape[1]
    nodes = rows_here * row_devices * col_devices
    scale = 1.0 / math.sqrt(rows_here)
    row_tiles = row_devices * rows_here // TILE
    col_tiles = col_devices * rows_here // TILE
    tile_block = tiles[0, 0]
    row_ids = tile_rows[0, 0]
    col_ids = tile_cols[0, 0]
    live_count = tile_count[0, 0]
    row_hi = row_ids // 2
    row_pos = jnp.where(row_ids % 2 == lax.axis_index("core"), row_hi, row_hi + row_tiles // 2)
    proj = jnp.dot(features, w_in, preferred_element_type=jnp.float32).astype(jnp.bfloat16)
    source = gather_rows(gather_rows(proj, "cz"), "cx")
    mine, other = tile_product(tile_block, row_pos, col_ids, live_count, (source,), row_tiles, False)
    summed = mine + swap_core(other)
    agg = scatter_rows(scatter_rows(summed, "y"), "zh")
    loss_sum, out_term, bias_term, grad_z = head_block(agg, bias, w_out, labels)
    gathered = gather_rows(grad_z, ("y", "zh"))
    sources = (gathered, swap_core(gathered))
    back_part = tile_product(tile_block, row_pos, col_ids, live_count, sources, col_tiles, True)
    grad_proj = scatter_rows(scatter_rows(back_part, "cx"), "cz").astype(jnp.bfloat16)
    in_term = jnp.einsum("nf,ng->fg", features, grad_proj, preferred_element_type=jnp.float32)
    extra = jnp.zeros((feat, 2), jnp.float32)
    extra = extra.at[:, 0].set(bias_term).at[0, 1].set(loss_sum)
    packed = jnp.concatenate([in_term, out_term, extra], axis=1)
    packed = reduce_all(packed, ("y", "zh", "cx", "cz"))
    grad_w_in = packed[:, :feat] * scale
    grad_w_out = packed[:, feat : feat + classes] * scale
    grad_bias = packed[:, feat + classes] * scale
    loss = packed[0, feat + classes + 1] / nodes
    grad_x = jnp.einsum("ng,fg->nf", grad_proj, w_in, preferred_element_type=jnp.float32).astype(
        jnp.bfloat16
    )
    return (loss, grad_x, grad_w_in, grad_w_out, grad_bias)


def solution(mesh):
    row_size, col_size = mesh.shape["row"], mesh.shape["col"]
    cz = 4 if col_size % 4 == 0 else 1
    fine = Mesh(
        mesh.devices.reshape(row_size // 4, 2, 2, col_size // cz, cz),
        ("y", "zh", "core", "cx", "cz"),
    )
    row, col = ("y", "zh", "core"), ("cx", "cz")
    placed = (
        P(row + col, None),
        P(),
        P(),
        P(),
        P(row, col, None, None, None),
        P(row, col, None),
        P(row, col, None),
        P(row, col),
        P(col + row),
    )
    return jax.shard_map(
        body,
        mesh=fine,
        in_specs=placed,
        out_specs=(P(), P(row + col, None), P(), P(), P()),
        check_vma=False,
    )
```

```python
import math

import jax
import jax.numpy as jnp
from jax import lax
from jax.experimental import pallas as pl
from jax.experimental.pallas import tpu as pltpu
from jax.sharding import Mesh, PartitionSpec as P

TILE = 128
CHUNK = 32


def _dense_kernel(transpose, rows_ref, cols_ref, count_ref, tiles_ref, src_a, src_b, out_a, out_b, dense_ref):
    step = pl.program_id(0)
    count = count_ref[0]

    @pl.when(step == 0)
    def _():
        dense_ref[...] = jnp.zeros_like(dense_ref)

    for j in range(CHUNK):
        slot = step * CHUNK + j

        @pl.when(slot < count)
        def _():
            at_row = pl.multiple_of(rows_ref[slot] * TILE, TILE)
            at_col = pl.multiple_of(cols_ref[slot] * TILE, TILE)
            dense_ref[pl.ds(at_row, TILE), pl.ds(at_col, TILE)] = tiles_ref[j]

    @pl.when(step == pl.num_programs(0) - 1)
    def _():
        half = dense_ref.shape[0] // 2
        if transpose:
            dims = (((0,), (0,)), ((), ()))
            res = lax.dot_general(src_a[...], dense_ref[:half, :], dims, preferred_element_type=jnp.float32)
            res += lax.dot_general(src_b[...], dense_ref[half:, :], dims, preferred_element_type=jnp.float32)
            out_a[...] = res
        else:
            src = src_a[...]
            out_a[...] = jnp.dot(dense_ref[:half, :], src, preferred_element_type=jnp.float32)
            out_b[...] = jnp.dot(dense_ref[half:, :], src, preferred_element_type=jnp.float32)


def tile_product(tile_block, row_ids, col_ids, live_count, sources, out_tiles, transpose):
    slots = tile_block.shape[0]
    width = sources[0].shape[1]
    steps = slots // CHUNK
    if transpose:
        src_tiles = 2 * sources[0].shape[0] // TILE
        dense_shape = (src_tiles * TILE, out_tiles * TILE)
        out_shapes = [(width, out_tiles * TILE), (8, 128)]
    else:
        sources = (sources[0], jnp.zeros((8, 128), sources[0].dtype))
        src_tiles = sources[0].shape[0] // TILE
        dense_shape = (out_tiles * TILE, src_tiles * TILE)
        out_shapes = [(out_tiles * TILE // 2, width)] * 2

    def tiles_map(i, rows, cols, count):
        last = jnp.maximum(count[0] - 1, 0) // CHUNK
        return (jnp.minimum(i, last), 0, 0)

    def whole(shape):
        return pl.BlockSpec(shape, lambda i, rows, cols, count: (0, 0))

    grid_spec = pltpu.PrefetchScalarGridSpec(
        num_scalar_prefetch=3,
        grid=(steps,),
        in_specs=[pl.BlockSpec((CHUNK, TILE, TILE), tiles_map)] + [whole(x.shape) for x in sources],
        out_specs=[whole(shape) for shape in out_shapes],
        scratch_shapes=[pltpu.VMEM(dense_shape, jnp.bfloat16)],
    )
    first, second = pl.pallas_call(
        lambda *refs: _dense_kernel(transpose, *refs),
        grid_spec=grid_spec,
        out_shape=[jax.ShapeDtypeStruct(shape, jnp.float32) for shape in out_shapes],
        compiler_params=pltpu.CompilerParams(dimension_semantics=("arbitrary",)),
    )(row_ids, col_ids, live_count.reshape(1), tile_block, *sources)
    if transpose:
        return first.T
    return first, second


def gather_rows(x, axis):
    n = lax.psum(1, axis)
    spread = jnp.broadcast_to(x[None], (n,) + x.shape)
    got = lax.all_to_all(spread, axis, 0, 0, tiled=False)
    return got.reshape(n * x.shape[0], x.shape[1])


def scatter_rows(x, axis):
    n = lax.psum(1, axis)
    got = lax.all_to_all(x.reshape(n, -1, x.shape[1]), axis, 0, 0, tiled=False)
    return jnp.sum(got, axis=0)


def swap_core(x, axis="core"):
    return lax.ppermute(x, axis, [(0, 1), (1, 0)])


def pair_scatter(x, axis):
    half = x.shape[0] // 2
    me = lax.axis_index(axis)
    mine = lax.dynamic_slice_in_dim(x, me * half, half, 0)
    other = lax.dynamic_slice_in_dim(x, (1 - me) * half, half, 0)
    return mine + swap_core(other, axis)


def pair_gather(x, axis):
    other = swap_core(x, axis)
    first = lax.axis_index(axis) == 0
    return jnp.where(first, jnp.concatenate([x, other]), jnp.concatenate([other, x]))


def reduce_all(x, axes):
    half = x.shape[0] // 2
    first = lax.axis_index("core") == 0
    mine = jnp.where(first, x[:half], x[half:])
    other = jnp.where(first, x[half:], x[:half])
    summed = mine + swap_core(other)
    summed = gather_rows(scatter_rows(summed, axes), axes)
    partner = swap_core(summed)
    return jnp.where(first, jnp.concatenate([summed, partner]), jnp.concatenate([partner, summed]))

def head_block(agg, bias, w_out, node_labels):
    pre_act = agg + bias[None, :]
    squash = jax.nn.sigmoid(pre_act)
    hidden = (pre_act * squash).astype(jnp.bfloat16)
    logits = jnp.dot(hidden, w_out, preferred_element_type=jnp.float32)
    top_val = jnp.max(logits, axis=1)
    lse = top_val + jnp.log(jnp.sum(jnp.exp(logits - top_val[:, None]), axis=1))
    onehot = (jnp.arange(w_out.shape[1], dtype=jnp.int32)[None, :] == node_labels[:, None]).astype(
        jnp.float32
    )
    picked = jnp.sum(logits * onehot, axis=1)
    loss_sum = jnp.sum(lse - picked)
    dlog = (jnp.exp(logits - lse[:, None]) - onehot).astype(jnp.bfloat16)
    out_term = jnp.einsum("nf,nc->fc", hidden, dlog, preferred_element_type=jnp.float32)
    d_hidden = jnp.einsum("nc,fc->nf", dlog, w_out, preferred_element_type=jnp.float32)
    grad_z = (d_hidden * squash * (1.0 + pre_act * (1.0 - squash))).astype(jnp.bfloat16)
    bias_term = jnp.sum(grad_z.astype(jnp.float32), axis=0)
    return (loss_sum, out_term, bias_term, grad_z)


def body(features, w_in, bias, w_out, tiles, tile_rows, tile_cols, tile_count, labels):
    row_devices = lax.psum(1, ("y", "zh", "core"))
    col_devices = lax.psum(1, ("cx", "cz"))
    rows_here = features.shape[0]
    feat = features.shape[1]
    classes = w_out.shape[1]
    nodes = rows_here * row_devices * col_devices
    scale = 1.0 / math.sqrt(rows_here)
    row_tiles = row_devices * rows_here // TILE
    col_tiles = col_devices * rows_here // TILE
    tile_block = tiles[0, 0]
    row_ids = tile_rows[0, 0]
    col_ids = tile_cols[0, 0]
    live_count = tile_count[0, 0]
    row_hi = row_ids // 2
    row_pos = jnp.where(row_ids % 2 == lax.axis_index("core"), row_hi, row_hi + row_tiles // 2)
    proj = jnp.dot(features, w_in, preferred_element_type=jnp.float32).astype(jnp.bfloat16)
    source = gather_rows(gather_rows(proj, "cz"), "cx")
    mine, other = tile_product(tile_block, row_pos, col_ids, live_count, (source,), row_tiles, False)
    summed = mine + swap_core(other)
    agg = pair_scatter(scatter_rows(summed, "y"), "zh")
    loss_sum, out_term, bias_term, grad_z = head_block(agg, bias, w_out, labels)
    gathered = gather_rows(pair_gather(grad_z, "zh"), "y")
    sources = (gathered, swap_core(gathered))
    back_part = tile_product(tile_block, row_pos, col_ids, live_count, sources, col_tiles, True)
    grad_proj = scatter_rows(scatter_rows(back_part, "cx"), "cz").astype(jnp.bfloat16)
    in_term = jnp.einsum("nf,ng->fg", features, grad_proj, preferred_element_type=jnp.float32)
    extra = jnp.zeros((feat, 2), jnp.float32)
    extra = extra.at[:, 0].set(bias_term).at[0, 1].set(loss_sum)
    packed = jnp.concatenate([in_term, out_term, extra], axis=1)
    packed = reduce_all(packed, ("y", "zh", "cx", "cz"))
    grad_w_in = packed[:, :feat] * scale
    grad_w_out = packed[:, feat : feat + classes] * scale
    grad_bias = packed[:, feat + classes] * scale
    loss = packed[0, feat + classes + 1] / nodes
    grad_x = jnp.einsum("ng,fg->nf", grad_proj, w_in, preferred_element_type=jnp.float32).astype(
        jnp.bfloat16
    )
    return (loss, grad_x, grad_w_in, grad_w_out, grad_bias)


def solution(mesh):
    row_size, col_size = mesh.shape["row"], mesh.shape["col"]
    cz = 4 if col_size % 4 == 0 else 1
    fine = Mesh(
        mesh.devices.reshape(row_size // 4, 2, 2, col_size // cz, cz),
        ("y", "zh", "core", "cx", "cz"),
    )
    row, col = ("y", "zh", "core"), ("cx", "cz")
    placed = (
        P(row + col, None),
        P(),
        P(),
        P(),
        P(row, col, None, None, None),
        P(row, col, None),
        P(row, col, None),
        P(row, col),
        P(col + row),
    )
    return jax.shard_map(
        body,
        mesh=fine,
        in_specs=placed,
        out_specs=(P(), P(row + col, None), P(), P(), P()),
        check_vma=False,
    )
```

```python
import math

import jax
import jax.numpy as jnp
from jax import lax
from jax.experimental import pallas as pl
from jax.experimental.pallas import tpu as pltpu
from jax.sharding import Mesh, PartitionSpec as P

TILE = 128
CHUNK = 32


def _dense_kernel(transpose, rows_ref, cols_ref, count_ref, tiles_ref, src_a, src_b, out_a, out_b, dense_ref):
    step = pl.program_id(0)
    count = count_ref[0]

    @pl.when(step == 0)
    def _():
        dense_ref[...] = jnp.zeros_like(dense_ref)

    for j in range(CHUNK):
        slot = step * CHUNK + j

        @pl.when(slot < count)
        def _():
            at_row = pl.multiple_of(rows_ref[slot] * TILE, TILE)
            at_col = pl.multiple_of(cols_ref[slot] * TILE, TILE)
            dense_ref[pl.ds(at_row, TILE), pl.ds(at_col, TILE)] = tiles_ref[j]

    @pl.when(step == pl.num_programs(0) - 1)
    def _():
        half = dense_ref.shape[0] // 2
        if transpose:
            dims = (((0,), (0,)), ((), ()))
            res = lax.dot_general(src_a[...], dense_ref[:half, :], dims, preferred_element_type=jnp.float32)
            res += lax.dot_general(src_b[...], dense_ref[half:, :], dims, preferred_element_type=jnp.float32)
            out_a[...] = res
        else:
            src = src_a[...]
            out_a[...] = jnp.dot(dense_ref[:half, :], src, preferred_element_type=jnp.float32)
            out_b[...] = jnp.dot(dense_ref[half:, :], src, preferred_element_type=jnp.float32)


def tile_product(tile_block, row_ids, col_ids, live_count, sources, out_tiles, transpose):
    slots = tile_block.shape[0]
    width = sources[0].shape[1]
    steps = slots // CHUNK
    if transpose:
        src_tiles = 2 * sources[0].shape[0] // TILE
        dense_shape = (src_tiles * TILE, out_tiles * TILE)
        out_shapes = [(width, out_tiles * TILE), (8, 128)]
    else:
        sources = (sources[0], jnp.zeros((8, 128), sources[0].dtype))
        src_tiles = sources[0].shape[0] // TILE
        dense_shape = (out_tiles * TILE, src_tiles * TILE)
        out_shapes = [(out_tiles * TILE // 2, width)] * 2

    def tiles_map(i, rows, cols, count):
        last = jnp.maximum(count[0] - 1, 0) // CHUNK
        return (jnp.minimum(i, last), 0, 0)

    def whole(shape):
        return pl.BlockSpec(shape, lambda i, rows, cols, count: (0, 0))

    grid_spec = pltpu.PrefetchScalarGridSpec(
        num_scalar_prefetch=3,
        grid=(steps,),
        in_specs=[pl.BlockSpec((CHUNK, TILE, TILE), tiles_map)] + [whole(x.shape) for x in sources],
        out_specs=[whole(shape) for shape in out_shapes],
        scratch_shapes=[pltpu.VMEM(dense_shape, jnp.bfloat16)],
    )
    first, second = pl.pallas_call(
        lambda *refs: _dense_kernel(transpose, *refs),
        grid_spec=grid_spec,
        out_shape=[jax.ShapeDtypeStruct(shape, jnp.float32) for shape in out_shapes],
        compiler_params=pltpu.CompilerParams(dimension_semantics=("arbitrary",)),
    )(row_ids, col_ids, live_count.reshape(1), tile_block, *sources)
    if transpose:
        return first.T
    return first, second


def gather_rows(x, axis):
    n = lax.psum(1, axis)
    spread = jnp.broadcast_to(x[None], (n,) + x.shape)
    got = lax.all_to_all(spread, axis, 0, 0, tiled=False)
    return got.reshape(n * x.shape[0], x.shape[1])


def scatter_rows(x, axis):
    n = lax.psum(1, axis)
    got = lax.all_to_all(x.reshape(n, -1, x.shape[1]), axis, 0, 0, tiled=False)
    return jnp.sum(got, axis=0)


def swap_core(x, axis="core"):
    return lax.ppermute(x, axis, [(0, 1), (1, 0)])


def pair_scatter(x, axis):
    half = x.shape[0] // 2
    me = lax.axis_index(axis)
    mine = lax.dynamic_slice_in_dim(x, me * half, half, 0)
    other = lax.dynamic_slice_in_dim(x, (1 - me) * half, half, 0)
    return mine + swap_core(other, axis)


def pair_gather(x, axis):
    other = swap_core(x, axis)
    first = lax.axis_index(axis) == 0
    return jnp.where(first, jnp.concatenate([x, other]), jnp.concatenate([other, x]))


def reduce_all(x, axes):
    half = x.shape[0] // 2
    first = lax.axis_index("core") == 0
    mine = jnp.where(first, x[:half], x[half:])
    other = jnp.where(first, x[half:], x[:half])
    summed = mine + swap_core(other)
    summed = gather_rows(scatter_rows(summed, axes), axes)
    partner = swap_core(summed)
    return jnp.where(first, jnp.concatenate([summed, partner]), jnp.concatenate([partner, summed]))

def head_block(agg, bias, w_out, node_labels):
    pre_act = agg + bias[None, :]
    squash = jax.nn.sigmoid(pre_act)
    hidden = (pre_act * squash).astype(jnp.bfloat16)
    logits = jnp.dot(hidden, w_out, preferred_element_type=jnp.float32)
    top_val = jnp.max(logits, axis=1)
    lse = top_val + jnp.log(jnp.sum(jnp.exp(logits - top_val[:, None]), axis=1))
    onehot = (jnp.arange(w_out.shape[1], dtype=jnp.int32)[None, :] == node_labels[:, None]).astype(
        jnp.float32
    )
    picked = jnp.sum(logits * onehot, axis=1)
    loss_sum = jnp.sum(lse - picked)
    dlog = (jnp.exp(logits - lse[:, None]) - onehot).astype(jnp.bfloat16)
    out_term = jnp.einsum("nf,nc->fc", hidden, dlog, preferred_element_type=jnp.float32)
    d_hidden = jnp.einsum("nc,fc->nf", dlog, w_out, preferred_element_type=jnp.float32)
    grad_z = (d_hidden * squash * (1.0 + pre_act * (1.0 - squash))).astype(jnp.bfloat16)
    bias_term = jnp.sum(grad_z.astype(jnp.float32), axis=0)
    return (loss_sum, out_term, bias_term, grad_z)


def body(features, w_in, bias, w_out, tiles, tile_rows, tile_cols, tile_count, labels):
    row_devices = lax.psum(1, ("y", "zh", "core"))
    col_devices = lax.psum(1, ("cx", "cz"))
    rows_here = features.shape[0]
    feat = features.shape[1]
    classes = w_out.shape[1]
    nodes = rows_here * row_devices * col_devices
    scale = 1.0 / math.sqrt(rows_here)
    row_tiles = row_devices * rows_here // TILE
    col_tiles = col_devices * rows_here // TILE
    tile_block = tiles[0, 0]
    row_ids = tile_rows[0, 0]
    col_ids = tile_cols[0, 0]
    live_count = tile_count[0, 0]
    row_hi = row_ids // 2
    row_pos = jnp.where(row_ids % 2 == lax.axis_index("core"), row_hi, row_hi + row_tiles // 2)
    proj = jnp.dot(features, w_in, preferred_element_type=jnp.float32).astype(jnp.bfloat16)
    source = gather_rows(gather_rows(proj, "cz"), "cx")
    mine, other = tile_product(tile_block, row_pos, col_ids, live_count, (source,), row_tiles, False)
    summed = mine + swap_core(other)
    agg = pair_scatter(scatter_rows(summed, "y"), "zh")
    loss_sum, out_term, bias_term, grad_z = head_block(agg, bias, w_out, labels)
    gathered = gather_rows(grad_z, ("y", "zh"))
    sources = (gathered, swap_core(gathered))
    back_part = tile_product(tile_block, row_pos, col_ids, live_count, sources, col_tiles, True)
    grad_proj = scatter_rows(scatter_rows(back_part, "cx"), "cz").astype(jnp.bfloat16)
    in_term = jnp.einsum("nf,ng->fg", features, grad_proj, preferred_element_type=jnp.float32)
    extra = jnp.zeros((feat, 2), jnp.float32)
    extra = extra.at[:, 0].set(bias_term).at[0, 1].set(loss_sum)
    packed = jnp.concatenate([in_term, out_term, extra], axis=1)
    packed = reduce_all(packed, ("y", "zh", "cx", "cz"))
    grad_w_in = packed[:, :feat] * scale
    grad_w_out = packed[:, feat : feat + classes] * scale
    grad_bias = packed[:, feat + classes] * scale
    loss = packed[0, feat + classes + 1] / nodes
    grad_x = jnp.einsum("ng,fg->nf", grad_proj, w_in, preferred_element_type=jnp.float32).astype(
        jnp.bfloat16
    )
    return (loss, grad_x, grad_w_in, grad_w_out, grad_bias)


def solution(mesh):
    row_size, col_size = mesh.shape["row"], mesh.shape["col"]
    cz = 4 if col_size % 4 == 0 else 1
    fine = Mesh(
        mesh.devices.reshape(row_size // 4, 2, 2, col_size // cz, cz),
        ("y", "zh", "core", "cx", "cz"),
    )
    row, col = ("y", "zh", "core"), ("cx", "cz")
    placed = (
        P(row + col, None),
        P(),
        P(),
        P(),
        P(row, col, None, None, None),
        P(row, col, None),
        P(row, col, None),
        P(row, col),
        P(col + row),
    )
    return jax.shard_map(
        body,
        mesh=fine,
        in_specs=placed,
        out_specs=(P(), P(row + col, None), P(), P(), P()),
        check_vma=False,
    )
```

```python
import math

import jax
import jax.numpy as jnp
from jax import lax
from jax.experimental import pallas as pl
from jax.experimental.pallas import tpu as pltpu
from jax.sharding import Mesh, PartitionSpec as P

TILE = 128
CHUNK = 32


def _dense_kernel(transpose, rows_ref, cols_ref, count_ref, tiles_ref, src_a, src_b, out_a, out_b, dense_ref):
    step = pl.program_id(0)
    count = count_ref[0]

    @pl.when(step == 0)
    def _():
        dense_ref[...] = jnp.zeros_like(dense_ref)

    for j in range(CHUNK):
        slot = step * CHUNK + j

        @pl.when(slot < count)
        def _():
            at_row = pl.multiple_of(rows_ref[slot] * TILE, TILE)
            at_col = pl.multiple_of(cols_ref[slot] * TILE, TILE)
            dense_ref[pl.ds(at_row, TILE), pl.ds(at_col, TILE)] = tiles_ref[j]

    @pl.when(step == pl.num_programs(0) - 1)
    def _():
        half = dense_ref.shape[0] // 2
        if transpose:
            dims = (((0,), (0,)), ((), ()))
            res = lax.dot_general(src_a[...], dense_ref[:half, :], dims, preferred_element_type=jnp.float32)
            res += lax.dot_general(src_b[...], dense_ref[half:, :], dims, preferred_element_type=jnp.float32)
            out_a[...] = res
        else:
            src = src_a[...]
            out_a[...] = jnp.dot(dense_ref[:half, :], src, preferred_element_type=jnp.float32)
            out_b[...] = jnp.dot(dense_ref[half:, :], src, preferred_element_type=jnp.float32)


def tile_product(tile_block, row_ids, col_ids, live_count, sources, out_tiles, transpose):
    slots = tile_block.shape[0]
    width = sources[0].shape[1]
    steps = slots // CHUNK
    if transpose:
        src_tiles = 2 * sources[0].shape[0] // TILE
        dense_shape = (src_tiles * TILE, out_tiles * TILE)
        out_shapes = [(width, out_tiles * TILE), (8, 128)]
    else:
        sources = (sources[0], jnp.zeros((8, 128), sources[0].dtype))
        src_tiles = sources[0].shape[0] // TILE
        dense_shape = (out_tiles * TILE, src_tiles * TILE)
        out_shapes = [(out_tiles * TILE // 2, width)] * 2

    def tiles_map(i, rows, cols, count):
        last = jnp.maximum(count[0] - 1, 0) // CHUNK
        return (jnp.minimum(i, last), 0, 0)

    def whole(shape):
        return pl.BlockSpec(shape, lambda i, rows, cols, count: (0, 0))

    grid_spec = pltpu.PrefetchScalarGridSpec(
        num_scalar_prefetch=3,
        grid=(steps,),
        in_specs=[pl.BlockSpec((CHUNK, TILE, TILE), tiles_map)] + [whole(x.shape) for x in sources],
        out_specs=[whole(shape) for shape in out_shapes],
        scratch_shapes=[pltpu.VMEM(dense_shape, jnp.bfloat16)],
    )
    first, second = pl.pallas_call(
        lambda *refs: _dense_kernel(transpose, *refs),
        grid_spec=grid_spec,
        out_shape=[jax.ShapeDtypeStruct(shape, jnp.float32) for shape in out_shapes],
        compiler_params=pltpu.CompilerParams(dimension_semantics=("arbitrary",)),
    )(row_ids, col_ids, live_count.reshape(1), tile_block, *sources)
    if transpose:
        return first.T
    return first, second


def gather_rows(x, axis):
    n = lax.psum(1, axis)
    spread = jnp.broadcast_to(x[None], (n,) + x.shape)
    got = lax.all_to_all(spread, axis, 0, 0, tiled=False)
    return got.reshape(n * x.shape[0], x.shape[1])


def scatter_rows(x, axis, kind=None):
    n = lax.psum(1, axis)
    sent = x.reshape(n, -1, x.shape[1])
    if kind is not None:
        sent = sent.astype(kind)
    got = lax.all_to_all(sent, axis, 0, 0, tiled=False)
    return jnp.sum(got.astype(jnp.float32), axis=0)


def swap_core(x, axis="core"):
    return lax.ppermute(x, axis, [(0, 1), (1, 0)])


def pair_scatter(x, axis):
    half = x.shape[0] // 2
    me = lax.axis_index(axis)
    mine = lax.dynamic_slice_in_dim(x, me * half, half, 0)
    other = lax.dynamic_slice_in_dim(x, (1 - me) * half, half, 0)
    return mine + swap_core(other, axis)


def pair_gather(x, axis):
    other = swap_core(x, axis)
    first = lax.axis_index(axis) == 0
    return jnp.where(first, jnp.concatenate([x, other]), jnp.concatenate([other, x]))


def reduce_all(x, axes):
    half = x.shape[0] // 2
    first = lax.axis_index("core") == 0
    mine = jnp.where(first, x[:half], x[half:])
    other = jnp.where(first, x[half:], x[:half])
    summed = mine + swap_core(other)
    summed = gather_rows(scatter_rows(summed, axes), axes)
    partner = swap_core(summed)
    return jnp.where(first, jnp.concatenate([summed, partner]), jnp.concatenate([partner, summed]))

def head_block(agg, bias, w_out, node_labels):
    pre_act = agg + bias[None, :]
    squash = jax.nn.sigmoid(pre_act)
    hidden = (pre_act * squash).astype(jnp.bfloat16)
    logits = jnp.dot(hidden, w_out, preferred_element_type=jnp.float32)
    top_val = jnp.max(logits, axis=1)
    lse = top_val + jnp.log(jnp.sum(jnp.exp(logits - top_val[:, None]), axis=1))
    onehot = (jnp.arange(w_out.shape[1], dtype=jnp.int32)[None, :] == node_labels[:, None]).astype(
        jnp.float32
    )
    picked = jnp.sum(logits * onehot, axis=1)
    loss_sum = jnp.sum(lse - picked)
    dlog = (jnp.exp(logits - lse[:, None]) - onehot).astype(jnp.bfloat16)
    out_term = jnp.einsum("nf,nc->fc", hidden, dlog, preferred_element_type=jnp.float32)
    d_hidden = jnp.einsum("nc,fc->nf", dlog, w_out, preferred_element_type=jnp.float32)
    grad_z = (d_hidden * squash * (1.0 + pre_act * (1.0 - squash))).astype(jnp.bfloat16)
    bias_term = jnp.sum(grad_z.astype(jnp.float32), axis=0)
    return (loss_sum, out_term, bias_term, grad_z)


def body(features, w_in, bias, w_out, tiles, tile_rows, tile_cols, tile_count, labels):
    row_devices = lax.psum(1, ("y", "zh", "core"))
    col_devices = lax.psum(1, ("cx", "cz"))
    rows_here = features.shape[0]
    feat = features.shape[1]
    classes = w_out.shape[1]
    nodes = rows_here * row_devices * col_devices
    scale = 1.0 / math.sqrt(rows_here)
    row_tiles = row_devices * rows_here // TILE
    col_tiles = col_devices * rows_here // TILE
    tile_block = tiles[0, 0]
    row_ids = tile_rows[0, 0]
    col_ids = tile_cols[0, 0]
    live_count = tile_count[0, 0]
    row_hi = row_ids // 2
    row_pos = jnp.where(row_ids % 2 == lax.axis_index("core"), row_hi, row_hi + row_tiles // 2)
    proj = jnp.dot(features, w_in, preferred_element_type=jnp.float32).astype(jnp.bfloat16)
    source = gather_rows(gather_rows(proj, "cz"), "cx")
    mine, other = tile_product(tile_block, row_pos, col_ids, live_count, (source,), row_tiles, False)
    summed = mine + swap_core(other)
    agg = pair_scatter(scatter_rows(summed, "y", jnp.bfloat16), "zh")
    loss_sum, out_term, bias_term, grad_z = head_block(agg, bias, w_out, labels)
    gathered = gather_rows(grad_z, ("y", "zh"))
    sources = (gathered, swap_core(gathered))
    back_part = tile_product(tile_block, row_pos, col_ids, live_count, sources, col_tiles, True)
    grad_proj = scatter_rows(scatter_rows(back_part, "cx"), "cz").astype(jnp.bfloat16)
    in_term = jnp.einsum("nf,ng->fg", features, grad_proj, preferred_element_type=jnp.float32)
    extra = jnp.zeros((feat, 2), jnp.float32)
    extra = extra.at[:, 0].set(bias_term).at[0, 1].set(loss_sum)
    packed = jnp.concatenate([in_term, out_term, extra], axis=1)
    packed = reduce_all(packed, ("y", "zh", "cx", "cz"))
    grad_w_in = packed[:, :feat] * scale
    grad_w_out = packed[:, feat : feat + classes] * scale
    grad_bias = packed[:, feat + classes] * scale
    loss = packed[0, feat + classes + 1] / nodes
    grad_x = jnp.einsum("ng,fg->nf", grad_proj, w_in, preferred_element_type=jnp.float32).astype(
        jnp.bfloat16
    )
    return (loss, grad_x, grad_w_in, grad_w_out, grad_bias)


def solution(mesh):
    row_size, col_size = mesh.shape["row"], mesh.shape["col"]
    cz = 4 if col_size % 4 == 0 else 1
    fine = Mesh(
        mesh.devices.reshape(row_size // 4, 2, 2, col_size // cz, cz),
        ("y", "zh", "core", "cx", "cz"),
    )
    row, col = ("y", "zh", "core"), ("cx", "cz")
    placed = (
        P(row + col, None),
        P(),
        P(),
        P(),
        P(row, col, None, None, None),
        P(row, col, None),
        P(row, col, None),
        P(row, col),
        P(col + row),
    )
    return jax.shard_map(
        body,
        mesh=fine,
        in_specs=placed,
        out_specs=(P(), P(row + col, None), P(), P(), P()),
        check_vma=False,
    )
```

```python
import math

import jax
import jax.numpy as jnp
from jax import lax
from jax.experimental import pallas as pl
from jax.experimental.pallas import tpu as pltpu
from jax.sharding import Mesh, PartitionSpec as P

TILE = 128
CHUNK = 32


def _dense_kernel(transpose, rows_ref, cols_ref, count_ref, tiles_ref, src_a, src_b, out_a, out_b, dense_ref):
    step = pl.program_id(0)
    count = count_ref[0]

    @pl.when(step == 0)
    def _():
        dense_ref[...] = jnp.zeros_like(dense_ref)

    for j in range(CHUNK):
        slot = step * CHUNK + j

        @pl.when(slot < count)
        def _():
            at_row = pl.multiple_of(rows_ref[slot] * TILE, TILE)
            at_col = pl.multiple_of(cols_ref[slot] * TILE, TILE)
            dense_ref[pl.ds(at_row, TILE), pl.ds(at_col, TILE)] = tiles_ref[j]

    @pl.when(step == pl.num_programs(0) - 1)
    def _():
        half = dense_ref.shape[0] // 2
        if transpose:
            dims = (((0,), (0,)), ((), ()))
            res = lax.dot_general(src_a[...], dense_ref[:half, :], dims, preferred_element_type=jnp.float32)
            res += lax.dot_general(src_b[...], dense_ref[half:, :], dims, preferred_element_type=jnp.float32)
            out_a[...] = res
        else:
            src = src_a[...]
            out_a[...] = jnp.dot(dense_ref[:half, :], src, preferred_element_type=jnp.float32)
            out_b[...] = jnp.dot(dense_ref[half:, :], src, preferred_element_type=jnp.float32)


def tile_product(tile_block, row_ids, col_ids, live_count, sources, out_tiles, transpose):
    slots = tile_block.shape[0]
    width = sources[0].shape[1]
    steps = slots // CHUNK
    if transpose:
        src_tiles = 2 * sources[0].shape[0] // TILE
        dense_shape = (src_tiles * TILE, out_tiles * TILE)
        out_shapes = [(width, out_tiles * TILE), (8, 128)]
    else:
        sources = (sources[0], jnp.zeros((8, 128), sources[0].dtype))
        src_tiles = sources[0].shape[0] // TILE
        dense_shape = (out_tiles * TILE, src_tiles * TILE)
        out_shapes = [(out_tiles * TILE // 2, width)] * 2

    def tiles_map(i, rows, cols, count):
        last = jnp.maximum(count[0] - 1, 0) // CHUNK
        return (jnp.minimum(i, last), 0, 0)

    def whole(shape):
        return pl.BlockSpec(shape, lambda i, rows, cols, count: (0, 0))

    grid_spec = pltpu.PrefetchScalarGridSpec(
        num_scalar_prefetch=3,
        grid=(steps,),
        in_specs=[pl.BlockSpec((CHUNK, TILE, TILE), tiles_map)] + [whole(x.shape) for x in sources],
        out_specs=[whole(shape) for shape in out_shapes],
        scratch_shapes=[pltpu.VMEM(dense_shape, jnp.bfloat16)],
    )
    first, second = pl.pallas_call(
        lambda *refs: _dense_kernel(transpose, *refs),
        grid_spec=grid_spec,
        out_shape=[jax.ShapeDtypeStruct(shape, jnp.float32) for shape in out_shapes],
        compiler_params=pltpu.CompilerParams(dimension_semantics=("arbitrary",)),
    )(row_ids, col_ids, live_count.reshape(1), tile_block, *sources)
    if transpose:
        return first.T
    return first, second


def gather_rows(x, axis):
    n = lax.psum(1, axis)
    spread = jnp.broadcast_to(x[None], (n,) + x.shape)
    got = lax.all_to_all(spread, axis, 0, 0, tiled=False)
    return got.reshape(n * x.shape[0], x.shape[1])


def scatter_rows(x, axis):
    n = lax.psum(1, axis)
    got = lax.all_to_all(x.reshape(n, -1, x.shape[1]), axis, 0, 0, tiled=False)
    return jnp.sum(got, axis=0)


def swap_core(x, axis="core"):
    return lax.ppermute(x, axis, [(0, 1), (1, 0)])


def ring_gather(x, axis):
    n = lax.psum(1, axis)
    me = lax.axis_index(axis)
    parts = [x] + [lax.ppermute(x, axis, [(i, (i + k) % n) for i in range(n)]) for k in range(1, n)]
    stacked = jnp.stack(parts[::-1])
    return jnp.roll(stacked, me + 1, axis=0).reshape(n * x.shape[0], x.shape[1])


def ring_scatter(x, axis):
    n = lax.psum(1, axis)
    me = lax.axis_index(axis)
    size = x.shape[0] // n
    total = lax.dynamic_slice_in_dim(x, me * size, size, 0)
    for k in range(1, n):
        piece = lax.dynamic_slice_in_dim(x, ((me + k) % n) * size, size, 0)
        total = total + lax.ppermute(piece, axis, [(i, (i + k) % n) for i in range(n)])
    return total


def pair_scatter(x, axis):
    half = x.shape[0] // 2
    me = lax.axis_index(axis)
    mine = lax.dynamic_slice_in_dim(x, me * half, half, 0)
    other = lax.dynamic_slice_in_dim(x, (1 - me) * half, half, 0)
    return mine + swap_core(other, axis)


def pair_gather(x, axis):
    other = swap_core(x, axis)
    first = lax.axis_index(axis) == 0
    return jnp.where(first, jnp.concatenate([x, other]), jnp.concatenate([other, x]))


def reduce_all(x, axes):
    half = x.shape[0] // 2
    first = lax.axis_index("core") == 0
    mine = jnp.where(first, x[:half], x[half:])
    other = jnp.where(first, x[half:], x[:half])
    summed = mine + swap_core(other)
    summed = gather_rows(scatter_rows(summed, axes), axes)
    partner = swap_core(summed)
    return jnp.where(first, jnp.concatenate([summed, partner]), jnp.concatenate([partner, summed]))

def head_block(agg, bias, w_out, node_labels):
    pre_act = agg + bias[None, :]
    squash = jax.nn.sigmoid(pre_act)
    hidden = (pre_act * squash).astype(jnp.bfloat16)
    logits = jnp.dot(hidden, w_out, preferred_element_type=jnp.float32)
    top_val = jnp.max(logits, axis=1)
    lse = top_val + jnp.log(jnp.sum(jnp.exp(logits - top_val[:, None]), axis=1))
    onehot = (jnp.arange(w_out.shape[1], dtype=jnp.int32)[None, :] == node_labels[:, None]).astype(
        jnp.float32
    )
    picked = jnp.sum(logits * onehot, axis=1)
    loss_sum = jnp.sum(lse - picked)
    dlog = (jnp.exp(logits - lse[:, None]) - onehot).astype(jnp.bfloat16)
    out_term = jnp.einsum("nf,nc->fc", hidden, dlog, preferred_element_type=jnp.float32)
    d_hidden = jnp.einsum("nc,fc->nf", dlog, w_out, preferred_element_type=jnp.float32)
    grad_z = (d_hidden * squash * (1.0 + pre_act * (1.0 - squash))).astype(jnp.bfloat16)
    bias_term = jnp.sum(grad_z.astype(jnp.float32), axis=0)
    return (loss_sum, out_term, bias_term, grad_z)


def body(features, w_in, bias, w_out, tiles, tile_rows, tile_cols, tile_count, labels):
    row_devices = lax.psum(1, ("y", "zh", "core"))
    col_devices = lax.psum(1, ("cx", "cz"))
    rows_here = features.shape[0]
    feat = features.shape[1]
    classes = w_out.shape[1]
    nodes = rows_here * row_devices * col_devices
    scale = 1.0 / math.sqrt(rows_here)
    row_tiles = row_devices * rows_here // TILE
    col_tiles = col_devices * rows_here // TILE
    tile_block = tiles[0, 0]
    row_ids = tile_rows[0, 0]
    col_ids = tile_cols[0, 0]
    live_count = tile_count[0, 0]
    row_hi = row_ids // 2
    row_pos = jnp.where(row_ids % 2 == lax.axis_index("core"), row_hi, row_hi + row_tiles // 2)
    proj = jnp.dot(features, w_in, preferred_element_type=jnp.float32).astype(jnp.bfloat16)
    source = ring_gather(ring_gather(proj, "cz"), "cx")
    mine, other = tile_product(tile_block, row_pos, col_ids, live_count, (source,), row_tiles, False)
    summed = mine + swap_core(other)
    agg = pair_scatter(scatter_rows(summed, "y"), "zh")
    loss_sum, out_term, bias_term, grad_z = head_block(agg, bias, w_out, labels)
    gathered = gather_rows(grad_z, ("y", "zh"))
    sources = (gathered, swap_core(gathered))
    back_part = tile_product(tile_block, row_pos, col_ids, live_count, sources, col_tiles, True)
    grad_proj = ring_scatter(ring_scatter(back_part, "cx"), "cz").astype(jnp.bfloat16)
    in_term = jnp.einsum("nf,ng->fg", features, grad_proj, preferred_element_type=jnp.float32)
    extra = jnp.zeros((feat, 2), jnp.float32)
    extra = extra.at[:, 0].set(bias_term).at[0, 1].set(loss_sum)
    packed = jnp.concatenate([in_term, out_term, extra], axis=1)
    packed = reduce_all(packed, ("y", "zh", "cx", "cz"))
    grad_w_in = packed[:, :feat] * scale
    grad_w_out = packed[:, feat : feat + classes] * scale
    grad_bias = packed[:, feat + classes] * scale
    loss = packed[0, feat + classes + 1] / nodes
    grad_x = jnp.einsum("ng,fg->nf", grad_proj, w_in, preferred_element_type=jnp.float32).astype(
        jnp.bfloat16
    )
    return (loss, grad_x, grad_w_in, grad_w_out, grad_bias)


def solution(mesh):
    row_size, col_size = mesh.shape["row"], mesh.shape["col"]
    cz = 4 if col_size % 4 == 0 else 1
    fine = Mesh(
        mesh.devices.reshape(row_size // 4, 2, 2, col_size // cz, cz),
        ("y", "zh", "core", "cx", "cz"),
    )
    row, col = ("y", "zh", "core"), ("cx", "cz")
    placed = (
        P(row + col, None),
        P(),
        P(),
        P(),
        P(row, col, None, None, None),
        P(row, col, None),
        P(row, col, None),
        P(row, col),
        P(col + row),
    )
    return jax.shard_map(
        body,
        mesh=fine,
        in_specs=placed,
        out_specs=(P(), P(row + col, None), P(), P(), P()),
        check_vma=False,
    )
```

```python
import math

import jax
import jax.numpy as jnp
from jax import lax
from jax.experimental import pallas as pl
from jax.experimental.pallas import tpu as pltpu
from jax.sharding import Mesh, PartitionSpec as P

TILE = 128
CHUNK = 32


def _dense_kernel(transpose, rows_ref, cols_ref, count_ref, tiles_ref, src_a, src_b, out_a, out_b, dense_ref):
    step = pl.program_id(0)
    count = count_ref[0]

    @pl.when(step == 0)
    def _():
        dense_ref[...] = jnp.zeros_like(dense_ref)

    for j in range(CHUNK):
        slot = step * CHUNK + j

        @pl.when(slot < count)
        def _():
            at_row = pl.multiple_of(rows_ref[slot] * TILE, TILE)
            at_col = pl.multiple_of(cols_ref[slot] * TILE, TILE)
            dense_ref[pl.ds(at_row, TILE), pl.ds(at_col, TILE)] = tiles_ref[j]

    @pl.when(step == pl.num_programs(0) - 1)
    def _():
        half = dense_ref.shape[0] // 2
        if transpose:
            dims = (((0,), (0,)), ((), ()))
            res = lax.dot_general(src_a[...], dense_ref[:half, :], dims, preferred_element_type=jnp.float32)
            res += lax.dot_general(src_b[...], dense_ref[half:, :], dims, preferred_element_type=jnp.float32)
            out_a[...] = res
        else:
            src = src_a[...]
            out_a[...] = jnp.dot(dense_ref[:half, :], src, preferred_element_type=jnp.float32)
            out_b[...] = jnp.dot(dense_ref[half:, :], src, preferred_element_type=jnp.float32)


def tile_product(tile_block, row_ids, col_ids, live_count, sources, out_tiles, transpose):
    slots = tile_block.shape[0]
    width = sources[0].shape[1]
    steps = slots // CHUNK
    if transpose:
        src_tiles = 2 * sources[0].shape[0] // TILE
        dense_shape = (src_tiles * TILE, out_tiles * TILE)
        out_shapes = [(width, out_tiles * TILE), (8, 128)]
    else:
        sources = (sources[0], jnp.zeros((8, 128), sources[0].dtype))
        src_tiles = sources[0].shape[0] // TILE
        dense_shape = (out_tiles * TILE, src_tiles * TILE)
        out_shapes = [(out_tiles * TILE // 2, width)] * 2

    def tiles_map(i, rows, cols, count):
        last = jnp.maximum(count[0] - 1, 0) // CHUNK
        return (jnp.minimum(i, last), 0, 0)

    def whole(shape):
        return pl.BlockSpec(shape, lambda i, rows, cols, count: (0, 0))

    grid_spec = pltpu.PrefetchScalarGridSpec(
        num_scalar_prefetch=3,
        grid=(steps,),
        in_specs=[pl.BlockSpec((CHUNK, TILE, TILE), tiles_map)] + [whole(x.shape) for x in sources],
        out_specs=[whole(shape) for shape in out_shapes],
        scratch_shapes=[pltpu.VMEM(dense_shape, jnp.bfloat16)],
    )
    first, second = pl.pallas_call(
        lambda *refs: _dense_kernel(transpose, *refs),
        grid_spec=grid_spec,
        out_shape=[jax.ShapeDtypeStruct(shape, jnp.float32) for shape in out_shapes],
        compiler_params=pltpu.CompilerParams(dimension_semantics=("arbitrary",)),
    )(row_ids, col_ids, live_count.reshape(1), tile_block, *sources)
    if transpose:
        return first.T
    return first, second


def gather_rows(x, axis):
    n = lax.psum(1, axis)
    spread = jnp.broadcast_to(x[None], (n,) + x.shape)
    got = lax.all_to_all(spread, axis, 0, 0, tiled=False)
    return got.reshape(n * x.shape[0], x.shape[1])


def scatter_rows(x, axis):
    n = lax.psum(1, axis)
    got = lax.all_to_all(x.reshape(n, -1, x.shape[1]), axis, 0, 0, tiled=False)
    return jnp.sum(got, axis=0)


def swap_core(x, axis="core"):
    return lax.ppermute(x, axis, [(0, 1), (1, 0)])


def ring_gather(x, axis):
    n = lax.psum(1, axis)
    me = lax.axis_index(axis)
    parts = [x] + [lax.ppermute(x, axis, [(i, (i + k) % n) for i in range(n)]) for k in range(1, n)]
    stacked = jnp.stack(parts[::-1])
    return jnp.roll(stacked, me + 1, axis=0).reshape(n * x.shape[0], x.shape[1])


def ring_scatter(x, axis):
    n = lax.psum(1, axis)
    me = lax.axis_index(axis)
    size = x.shape[0] // n
    total = lax.dynamic_slice_in_dim(x, me * size, size, 0)
    for k in range(1, n):
        piece = lax.dynamic_slice_in_dim(x, ((me + k) % n) * size, size, 0)
        total = total + lax.ppermute(piece, axis, [(i, (i + k) % n) for i in range(n)])
    return total


def pair_scatter(x, axis):
    half = x.shape[0] // 2
    me = lax.axis_index(axis)
    mine = lax.dynamic_slice_in_dim(x, me * half, half, 0)
    other = lax.dynamic_slice_in_dim(x, (1 - me) * half, half, 0)
    return mine + swap_core(other, axis)


def pair_gather(x, axis):
    other = swap_core(x, axis)
    first = lax.axis_index(axis) == 0
    return jnp.where(first, jnp.concatenate([x, other]), jnp.concatenate([other, x]))


def reduce_all(x, axes):
    half = x.shape[0] // 2
    first = lax.axis_index("core") == 0
    mine = jnp.where(first, x[:half], x[half:])
    other = jnp.where(first, x[half:], x[:half])
    summed = mine + swap_core(other)
    summed = gather_rows(scatter_rows(summed, axes), axes)
    partner = swap_core(summed)
    return jnp.where(first, jnp.concatenate([summed, partner]), jnp.concatenate([partner, summed]))

def head_block(agg, bias, w_out, node_labels):
    pre_act = agg + bias[None, :]
    squash = jax.nn.sigmoid(pre_act)
    hidden = (pre_act * squash).astype(jnp.bfloat16)
    logits = jnp.dot(hidden, w_out, preferred_element_type=jnp.float32)
    top_val = jnp.max(logits, axis=1)
    lse = top_val + jnp.log(jnp.sum(jnp.exp(logits - top_val[:, None]), axis=1))
    onehot = (jnp.arange(w_out.shape[1], dtype=jnp.int32)[None, :] == node_labels[:, None]).astype(
        jnp.float32
    )
    picked = jnp.sum(logits * onehot, axis=1)
    loss_sum = jnp.sum(lse - picked)
    dlog = (jnp.exp(logits - lse[:, None]) - onehot).astype(jnp.bfloat16)
    out_term = jnp.einsum("nf,nc->fc", hidden, dlog, preferred_element_type=jnp.float32)
    d_hidden = jnp.einsum("nc,fc->nf", dlog, w_out, preferred_element_type=jnp.float32)
    grad_z = (d_hidden * squash * (1.0 + pre_act * (1.0 - squash))).astype(jnp.bfloat16)
    bias_term = jnp.sum(grad_z.astype(jnp.float32), axis=0)
    return (loss_sum, out_term, bias_term, grad_z)


def body(features, w_in, bias, w_out, tiles, tile_rows, tile_cols, tile_count, labels):
    row_devices = lax.psum(1, ("y", "zh", "core"))
    col_devices = lax.psum(1, ("cx", "cz"))
    rows_here = features.shape[0]
    feat = features.shape[1]
    classes = w_out.shape[1]
    nodes = rows_here * row_devices * col_devices
    scale = 1.0 / math.sqrt(rows_here)
    row_tiles = row_devices * rows_here // TILE
    col_tiles = col_devices * rows_here // TILE
    tile_block = tiles[0, 0]
    row_ids = tile_rows[0, 0]
    col_ids = tile_cols[0, 0]
    live_count = tile_count[0, 0]
    row_hi = row_ids // 2
    row_pos = jnp.where(row_ids % 2 == lax.axis_index("core"), row_hi, row_hi + row_tiles // 2)
    proj = jnp.dot(features, w_in, preferred_element_type=jnp.float32).astype(jnp.bfloat16)
    source = ring_gather(ring_gather(proj, "cz"), "cx")
    mine, other = tile_product(tile_block, row_pos, col_ids, live_count, (source,), row_tiles, False)
    summed = mine + swap_core(other)
    agg = pair_scatter(ring_scatter(summed, "y"), "zh")
    loss_sum, out_term, bias_term, grad_z = head_block(agg, bias, w_out, labels)
    gathered = ring_gather(ring_gather(grad_z, "zh"), "y")
    sources = (gathered, swap_core(gathered))
    back_part = tile_product(tile_block, row_pos, col_ids, live_count, sources, col_tiles, True)
    grad_proj = ring_scatter(ring_scatter(back_part, "cx"), "cz").astype(jnp.bfloat16)
    in_term = jnp.einsum("nf,ng->fg", features, grad_proj, preferred_element_type=jnp.float32)
    extra = jnp.zeros((feat, 2), jnp.float32)
    extra = extra.at[:, 0].set(bias_term).at[0, 1].set(loss_sum)
    packed = jnp.concatenate([in_term, out_term, extra], axis=1)
    packed = reduce_all(packed, ("y", "zh", "cx", "cz"))
    grad_w_in = packed[:, :feat] * scale
    grad_w_out = packed[:, feat : feat + classes] * scale
    grad_bias = packed[:, feat + classes] * scale
    loss = packed[0, feat + classes + 1] / nodes
    grad_x = jnp.einsum("ng,fg->nf", grad_proj, w_in, preferred_element_type=jnp.float32).astype(
        jnp.bfloat16
    )
    return (loss, grad_x, grad_w_in, grad_w_out, grad_bias)


def solution(mesh):
    row_size, col_size = mesh.shape["row"], mesh.shape["col"]
    cz = 4 if col_size % 4 == 0 else 1
    fine = Mesh(
        mesh.devices.reshape(row_size // 4, 2, 2, col_size // cz, cz),
        ("y", "zh", "core", "cx", "cz"),
    )
    row, col = ("y", "zh", "core"), ("cx", "cz")
    placed = (
        P(row + col, None),
        P(),
        P(),
        P(),
        P(row, col, None, None, None),
        P(row, col, None),
        P(row, col, None),
        P(row, col),
        P(col + row),
    )
    return jax.shard_map(
        body,
        mesh=fine,
        in_specs=placed,
        out_specs=(P(), P(row + col, None), P(), P(), P()),
        check_vma=False,
    )
```

```python
import math

import jax
import jax.numpy as jnp
from jax import lax
from jax.experimental import pallas as pl
from jax.experimental.pallas import tpu as pltpu
from jax.sharding import Mesh, PartitionSpec as P

TILE = 128
CHUNK = 32


def _dense_kernel(transpose, rows_ref, cols_ref, count_ref, tiles_ref, src_a, src_b, out_a, out_b, dense_ref):
    step = pl.program_id(0)
    count = count_ref[0]

    @pl.when(step == 0)
    def _():
        dense_ref[...] = jnp.zeros_like(dense_ref)

    for j in range(CHUNK):
        slot = step * CHUNK + j

        @pl.when(slot < count)
        def _():
            at_row = pl.multiple_of(rows_ref[slot] * TILE, TILE)
            at_col = pl.multiple_of(cols_ref[slot] * TILE, TILE)
            dense_ref[pl.ds(at_row, TILE), pl.ds(at_col, TILE)] = tiles_ref[j]

    @pl.when(step == pl.num_programs(0) - 1)
    def _():
        half = dense_ref.shape[0] // 2
        if transpose:
            dims = (((0,), (0,)), ((), ()))
            res = lax.dot_general(src_a[...], dense_ref[:half, :], dims, preferred_element_type=jnp.float32)
            res += lax.dot_general(src_b[...], dense_ref[half:, :], dims, preferred_element_type=jnp.float32)
            out_a[...] = res
        else:
            src = src_a[...]
            out_a[...] = jnp.dot(dense_ref[:half, :], src, preferred_element_type=jnp.float32)
            out_b[...] = jnp.dot(dense_ref[half:, :], src, preferred_element_type=jnp.float32)


def tile_product(tile_block, row_ids, col_ids, live_count, sources, out_tiles, transpose):
    slots = tile_block.shape[0]
    width = sources[0].shape[1]
    steps = slots // CHUNK
    if transpose:
        src_tiles = 2 * sources[0].shape[0] // TILE
        dense_shape = (src_tiles * TILE, out_tiles * TILE)
        out_shapes = [(width, out_tiles * TILE), (8, 128)]
    else:
        sources = (sources[0], jnp.zeros((8, 128), sources[0].dtype))
        src_tiles = sources[0].shape[0] // TILE
        dense_shape = (out_tiles * TILE, src_tiles * TILE)
        out_shapes = [(out_tiles * TILE // 2, width)] * 2

    def tiles_map(i, rows, cols, count):
        last = jnp.maximum(count[0] - 1, 0) // CHUNK
        return (jnp.minimum(i, last), 0, 0)

    def whole(shape):
        return pl.BlockSpec(shape, lambda i, rows, cols, count: (0, 0))

    grid_spec = pltpu.PrefetchScalarGridSpec(
        num_scalar_prefetch=3,
        grid=(steps,),
        in_specs=[pl.BlockSpec((CHUNK, TILE, TILE), tiles_map)] + [whole(x.shape) for x in sources],
        out_specs=[whole(shape) for shape in out_shapes],
        scratch_shapes=[pltpu.VMEM(dense_shape, jnp.bfloat16)],
    )
    first, second = pl.pallas_call(
        lambda *refs: _dense_kernel(transpose, *refs),
        grid_spec=grid_spec,
        out_shape=[jax.ShapeDtypeStruct(shape, jnp.float32) for shape in out_shapes],
        compiler_params=pltpu.CompilerParams(dimension_semantics=("arbitrary",)),
    )(row_ids, col_ids, live_count.reshape(1), tile_block, *sources)
    if transpose:
        return first.T
    return first, second


def gather_rows(x, axis):
    n = lax.psum(1, axis)
    spread = jnp.broadcast_to(x[None], (n,) + x.shape)
    got = lax.all_to_all(spread, axis, 0, 0, tiled=False)
    return got.reshape(n * x.shape[0], x.shape[1])


def scatter_rows(x, axis):
    n = lax.psum(1, axis)
    got = lax.all_to_all(x.reshape(n, -1, x.shape[1]), axis, 0, 0, tiled=False)
    return jnp.sum(got, axis=0)


def swap_core(x, axis="core"):
    return lax.ppermute(x, axis, [(0, 1), (1, 0)])


def ring_gather(x, axis):
    n = lax.psum(1, axis)
    me = lax.axis_index(axis)
    parts = [x] + [lax.ppermute(x, axis, [(i, (i + k) % n) for i in range(n)]) for k in range(1, n)]
    stacked = jnp.stack(parts[::-1])
    return jnp.roll(stacked, me + 1, axis=0).reshape(n * x.shape[0], x.shape[1])


def ring_scatter(x, axis):
    n = lax.psum(1, axis)
    me = lax.axis_index(axis)
    size = x.shape[0] // n
    total = lax.dynamic_slice_in_dim(x, me * size, size, 0)
    for k in range(1, n):
        piece = lax.dynamic_slice_in_dim(x, ((me + k) % n) * size, size, 0)
        total = total + lax.ppermute(piece, axis, [(i, (i + k) % n) for i in range(n)])
    return total


def pair_scatter(x, axis):
    half = x.shape[0] // 2
    me = lax.axis_index(axis)
    mine = lax.dynamic_slice_in_dim(x, me * half, half, 0)
    other = lax.dynamic_slice_in_dim(x, (1 - me) * half, half, 0)
    return mine + swap_core(other, axis)


def pair_gather(x, axis):
    other = swap_core(x, axis)
    first = lax.axis_index(axis) == 0
    return jnp.where(first, jnp.concatenate([x, other]), jnp.concatenate([other, x]))


def reduce_all(x, axes):
    x = ring_scatter(pair_scatter(x, "core"), "cz")
    x = gather_rows(scatter_rows(x, axes), axes)
    return pair_gather(ring_gather(x, "cz"), "core")


def head_block(agg, bias, w_out, node_labels):
    pre_act = agg + bias[None, :]
    squash = jax.nn.sigmoid(pre_act)
    hidden = (pre_act * squash).astype(jnp.bfloat16)
    logits = jnp.dot(hidden, w_out, preferred_element_type=jnp.float32)
    top_val = jnp.max(logits, axis=1)
    lse = top_val + jnp.log(jnp.sum(jnp.exp(logits - top_val[:, None]), axis=1))
    onehot = (jnp.arange(w_out.shape[1], dtype=jnp.int32)[None, :] == node_labels[:, None]).astype(
        jnp.float32
    )
    picked = jnp.sum(logits * onehot, axis=1)
    loss_sum = jnp.sum(lse - picked)
    dlog = (jnp.exp(logits - lse[:, None]) - onehot).astype(jnp.bfloat16)
    out_term = jnp.einsum("nf,nc->fc", hidden, dlog, preferred_element_type=jnp.float32)
    d_hidden = jnp.einsum("nc,fc->nf", dlog, w_out, preferred_element_type=jnp.float32)
    grad_z = (d_hidden * squash * (1.0 + pre_act * (1.0 - squash))).astype(jnp.bfloat16)
    bias_term = jnp.sum(grad_z.astype(jnp.float32), axis=0)
    return (loss_sum, out_term, bias_term, grad_z)


def body(features, w_in, bias, w_out, tiles, tile_rows, tile_cols, tile_count, labels):
    row_devices = lax.psum(1, ("y", "zh", "core"))
    col_devices = lax.psum(1, ("cx", "cz"))
    rows_here = features.shape[0]
    feat = features.shape[1]
    classes = w_out.shape[1]
    nodes = rows_here * row_devices * col_devices
    scale = 1.0 / math.sqrt(rows_here)
    row_tiles = row_devices * rows_here // TILE
    col_tiles = col_devices * rows_here // TILE
    tile_block = tiles[0, 0]
    row_ids = tile_rows[0, 0]
    col_ids = tile_cols[0, 0]
    live_count = tile_count[0, 0]
    row_hi = row_ids // 2
    row_pos = jnp.where(row_ids % 2 == lax.axis_index("core"), row_hi, row_hi + row_tiles // 2)
    proj = jnp.dot(features, w_in, preferred_element_type=jnp.float32).astype(jnp.bfloat16)
    source = ring_gather(ring_gather(proj, "cz"), "cx")
    mine, other = tile_product(tile_block, row_pos, col_ids, live_count, (source,), row_tiles, False)
    summed = mine + swap_core(other)
    agg = pair_scatter(ring_scatter(summed, "y"), "zh")
    loss_sum, out_term, bias_term, grad_z = head_block(agg, bias, w_out, labels)
    gathered = ring_gather(ring_gather(grad_z, "zh"), "y")
    sources = (gathered, swap_core(gathered))
    back_part = tile_product(tile_block, row_pos, col_ids, live_count, sources, col_tiles, True)
    grad_proj = ring_scatter(ring_scatter(back_part, "cx"), "cz").astype(jnp.bfloat16)
    in_term = jnp.einsum("nf,ng->fg", features, grad_proj, preferred_element_type=jnp.float32)
    extra = jnp.zeros((feat, 2), jnp.float32)
    extra = extra.at[:, 0].set(bias_term).at[0, 1].set(loss_sum)
    packed = jnp.concatenate([in_term, out_term, extra], axis=1)
    packed = reduce_all(packed, ("y", "zh", "cx"))
    grad_w_in = packed[:, :feat] * scale
    grad_w_out = packed[:, feat : feat + classes] * scale
    grad_bias = packed[:, feat + classes] * scale
    loss = packed[0, feat + classes + 1] / nodes
    grad_x = jnp.einsum("ng,fg->nf", grad_proj, w_in, preferred_element_type=jnp.float32).astype(
        jnp.bfloat16
    )
    return (loss, grad_x, grad_w_in, grad_w_out, grad_bias)


def solution(mesh):
    row_size, col_size = mesh.shape["row"], mesh.shape["col"]
    cz = 4 if col_size % 4 == 0 else 1
    fine = Mesh(
        mesh.devices.reshape(row_size // 4, 2, 2, col_size // cz, cz),
        ("y", "zh", "core", "cx", "cz"),
    )
    row, col = ("y", "zh", "core"), ("cx", "cz")
    placed = (
        P(row + col, None),
        P(),
        P(),
        P(),
        P(row, col, None, None, None),
        P(row, col, None),
        P(row, col, None),
        P(row, col),
        P(col + row),
    )
    return jax.shard_map(
        body,
        mesh=fine,
        in_specs=placed,
        out_specs=(P(), P(row + col, None), P(), P(), P()),
        check_vma=False,
    )
```

```python
import math

import jax
import jax.numpy as jnp
from jax import lax
from jax.experimental import pallas as pl
from jax.experimental.pallas import tpu as pltpu
from jax.sharding import Mesh, PartitionSpec as P

TILE = 128
CHUNK = 32


def _dense_kernel(transpose, rows_ref, cols_ref, count_ref, tiles_ref, src_a, src_b, out_a, out_b, dense_ref):
    step = pl.program_id(0)
    count = count_ref[0]

    @pl.when(step == 0)
    def _():
        dense_ref[...] = jnp.zeros_like(dense_ref)

    for j in range(CHUNK):
        slot = step * CHUNK + j

        @pl.when(slot < count)
        def _():
            at_row = pl.multiple_of(rows_ref[slot] * TILE, TILE)
            at_col = pl.multiple_of(cols_ref[slot] * TILE, TILE)
            dense_ref[pl.ds(at_row, TILE), pl.ds(at_col, TILE)] = tiles_ref[j]

    @pl.when(step == pl.num_programs(0) - 1)
    def _():
        half = dense_ref.shape[0] // 2
        if transpose:
            dims = (((0,), (0,)), ((), ()))
            res = lax.dot_general(src_a[...], dense_ref[:half, :], dims, preferred_element_type=jnp.float32)
            res += lax.dot_general(src_b[...], dense_ref[half:, :], dims, preferred_element_type=jnp.float32)
            out_a[...] = res
        else:
            src = src_a[...]
            out_a[...] = jnp.dot(dense_ref[:half, :], src, preferred_element_type=jnp.float32)
            out_b[...] = jnp.dot(dense_ref[half:, :], src, preferred_element_type=jnp.float32)


def tile_product(tile_block, row_ids, col_ids, live_count, sources, out_tiles, transpose):
    slots = tile_block.shape[0]
    width = sources[0].shape[1]
    steps = slots // CHUNK
    if transpose:
        src_tiles = 2 * sources[0].shape[0] // TILE
        dense_shape = (src_tiles * TILE, out_tiles * TILE)
        out_shapes = [(width, out_tiles * TILE), (8, 128)]
    else:
        sources = (sources[0], jnp.zeros((8, 128), sources[0].dtype))
        src_tiles = sources[0].shape[0] // TILE
        dense_shape = (out_tiles * TILE, src_tiles * TILE)
        out_shapes = [(out_tiles * TILE // 2, width)] * 2

    def tiles_map(i, rows, cols, count):
        last = jnp.maximum(count[0] - 1, 0) // CHUNK
        return (jnp.minimum(i, last), 0, 0)

    def whole(shape):
        return pl.BlockSpec(shape, lambda i, rows, cols, count: (0, 0))

    grid_spec = pltpu.PrefetchScalarGridSpec(
        num_scalar_prefetch=3,
        grid=(steps,),
        in_specs=[pl.BlockSpec((CHUNK, TILE, TILE), tiles_map)] + [whole(x.shape) for x in sources],
        out_specs=[whole(shape) for shape in out_shapes],
        scratch_shapes=[pltpu.VMEM(dense_shape, jnp.bfloat16)],
    )
    first, second = pl.pallas_call(
        lambda *refs: _dense_kernel(transpose, *refs),
        grid_spec=grid_spec,
        out_shape=[jax.ShapeDtypeStruct(shape, jnp.float32) for shape in out_shapes],
        compiler_params=pltpu.CompilerParams(dimension_semantics=("arbitrary",)),
    )(row_ids, col_ids, live_count.reshape(1), tile_block, *sources)
    if transpose:
        return first.T
    return first, second


def gather_rows(x, axis):
    n = lax.psum(1, axis)
    spread = jnp.broadcast_to(x[None], (n,) + x.shape)
    got = lax.all_to_all(spread, axis, 0, 0, tiled=False)
    return got.reshape(n * x.shape[0], x.shape[1])


def scatter_rows(x, axis):
    n = lax.psum(1, axis)
    got = lax.all_to_all(x.reshape(n, -1, x.shape[1]), axis, 0, 0, tiled=False)
    return jnp.sum(got, axis=0)


def swap_core(x, axis="core"):
    return lax.ppermute(x, axis, [(0, 1), (1, 0)])


def ring_gather(x, axis):
    n = lax.psum(1, axis)
    me = lax.axis_index(axis)
    parts = [x] + [lax.ppermute(x, axis, [(i, (i + k) % n) for i in range(n)]) for k in range(1, n)]
    stacked = jnp.stack(parts[::-1])
    return jnp.roll(stacked, me + 1, axis=0).reshape(n * x.shape[0], x.shape[1])


def ring_scatter(x, axis):
    n = lax.psum(1, axis)
    me = lax.axis_index(axis)
    size = x.shape[0] // n
    total = lax.dynamic_slice_in_dim(x, me * size, size, 0)
    for k in range(1, n):
        piece = lax.dynamic_slice_in_dim(x, ((me + k) % n) * size, size, 0)
        total = total + lax.ppermute(piece, axis, [(i, (i + k) % n) for i in range(n)])
    return total


def pair_scatter(x, axis):
    half = x.shape[0] // 2
    me = lax.axis_index(axis)
    mine = lax.dynamic_slice_in_dim(x, me * half, half, 0)
    other = lax.dynamic_slice_in_dim(x, (1 - me) * half, half, 0)
    return mine + swap_core(other, axis)


def pair_gather(x, axis):
    other = swap_core(x, axis)
    first = lax.axis_index(axis) == 0
    return jnp.where(first, jnp.concatenate([x, other]), jnp.concatenate([other, x]))


def reduce_all(x, axes):
    half = x.shape[0] // 2
    first = lax.axis_index("core") == 0
    mine = jnp.where(first, x[:half], x[half:])
    other = jnp.where(first, x[half:], x[:half])
    summed = mine + swap_core(other)
    summed = gather_rows(scatter_rows(summed, axes), axes)
    partner = swap_core(summed)
    return jnp.where(first, jnp.concatenate([summed, partner]), jnp.concatenate([partner, summed]))

def head_block(agg, bias, w_out, node_labels):
    pre_act = agg + bias[None, :]
    squash = jax.nn.sigmoid(pre_act)
    hidden = (pre_act * squash).astype(jnp.bfloat16)
    logits = jnp.dot(hidden, w_out, preferred_element_type=jnp.float32)
    top_val = jnp.max(logits, axis=1)
    lse = top_val + jnp.log(jnp.sum(jnp.exp(logits - top_val[:, None]), axis=1))
    onehot = (jnp.arange(w_out.shape[1], dtype=jnp.int32)[None, :] == node_labels[:, None]).astype(
        jnp.float32
    )
    picked = jnp.sum(logits * onehot, axis=1)
    loss_sum = jnp.sum(lse - picked)
    dlog = (jnp.exp(logits - lse[:, None]) - onehot).astype(jnp.bfloat16)
    out_term = jnp.einsum("nf,nc->fc", hidden, dlog, preferred_element_type=jnp.float32)
    d_hidden = jnp.einsum("nc,fc->nf", dlog, w_out, preferred_element_type=jnp.float32)
    grad_z = (d_hidden * squash * (1.0 + pre_act * (1.0 - squash))).astype(jnp.bfloat16)
    bias_term = jnp.sum(grad_z.astype(jnp.float32), axis=0)
    return (loss_sum, out_term, bias_term, grad_z)


def body(features, w_in, bias, w_out, tiles, tile_rows, tile_cols, tile_count, labels):
    row_devices = lax.psum(1, ("y", "zh", "core"))
    col_devices = lax.psum(1, ("cx", "cz"))
    rows_here = features.shape[0]
    feat = features.shape[1]
    classes = w_out.shape[1]
    nodes = rows_here * row_devices * col_devices
    scale = 1.0 / math.sqrt(rows_here)
    row_tiles = row_devices * rows_here // TILE
    col_tiles = col_devices * rows_here // TILE
    tile_block = tiles[0, 0]
    row_ids = tile_rows[0, 0]
    col_ids = tile_cols[0, 0]
    live_count = tile_count[0, 0]
    row_hi = row_ids // 2
    row_pos = jnp.where(row_ids % 2 == lax.axis_index("core"), row_hi, row_hi + row_tiles // 2)
    proj = jnp.dot(features, w_in, preferred_element_type=jnp.float32).astype(jnp.bfloat16)
    source = ring_gather(ring_gather(proj, "cz"), "cx")
    mine, other = tile_product(tile_block, row_pos, col_ids, live_count, (source,), row_tiles, False)
    summed = mine + swap_core(other)
    agg = pair_scatter(ring_scatter(summed, "y"), "zh")
    loss_sum, out_term, bias_term, grad_z = head_block(agg, bias, w_out, labels)
    gathered = gather_rows(grad_z, ("y", "zh"))
    sources = (gathered, swap_core(gathered))
    back_part = tile_product(tile_block, row_pos, col_ids, live_count, sources, col_tiles, True)
    grad_proj = ring_scatter(ring_scatter(back_part, "cx"), "cz").astype(jnp.bfloat16)
    in_term = jnp.einsum("nf,ng->fg", features, grad_proj, preferred_element_type=jnp.float32)
    extra = jnp.zeros((feat, 2), jnp.float32)
    extra = extra.at[:, 0].set(bias_term).at[0, 1].set(loss_sum)
    packed = jnp.concatenate([in_term, out_term, extra], axis=1)
    packed = reduce_all(packed, ("y", "zh", "cx", "cz"))
    grad_w_in = packed[:, :feat] * scale
    grad_w_out = packed[:, feat : feat + classes] * scale
    grad_bias = packed[:, feat + classes] * scale
    loss = packed[0, feat + classes + 1] / nodes
    grad_x = jnp.einsum("ng,fg->nf", grad_proj, w_in, preferred_element_type=jnp.float32).astype(
        jnp.bfloat16
    )
    return (loss, grad_x, grad_w_in, grad_w_out, grad_bias)


def solution(mesh):
    row_size, col_size = mesh.shape["row"], mesh.shape["col"]
    cz = 4 if col_size % 4 == 0 else 1
    fine = Mesh(
        mesh.devices.reshape(row_size // 4, 2, 2, col_size // cz, cz),
        ("y", "zh", "core", "cx", "cz"),
    )
    row, col = ("y", "zh", "core"), ("cx", "cz")
    placed = (
        P(row + col, None),
        P(),
        P(),
        P(),
        P(row, col, None, None, None),
        P(row, col, None),
        P(row, col, None),
        P(row, col),
        P(col + row),
    )
    return jax.shard_map(
        body,
        mesh=fine,
        in_specs=placed,
        out_specs=(P(), P(row + col, None), P(), P(), P()),
        check_vma=False,
    )
```

```python
import math

import jax
import jax.numpy as jnp
from jax import lax
from jax.experimental import pallas as pl
from jax.experimental.pallas import tpu as pltpu
from jax.sharding import Mesh, PartitionSpec as P

TILE = 128
CHUNK = 64


def _dense_kernel(transpose, rows_ref, cols_ref, count_ref, tiles_ref, src_a, src_b, out_a, out_b, dense_ref):
    step = pl.program_id(0)
    count = count_ref[0]

    @pl.when(step == 0)
    def _():
        dense_ref[...] = jnp.zeros_like(dense_ref)

    for j in range(CHUNK):
        slot = step * CHUNK + j

        @pl.when(slot < count)
        def _():
            at_row = pl.multiple_of(rows_ref[slot] * TILE, TILE)
            at_col = pl.multiple_of(cols_ref[slot] * TILE, TILE)
            dense_ref[pl.ds(at_row, TILE), pl.ds(at_col, TILE)] = tiles_ref[j]

    @pl.when(step == pl.num_programs(0) - 1)
    def _():
        half = dense_ref.shape[0] // 2
        if transpose:
            dims = (((0,), (0,)), ((), ()))
            res = lax.dot_general(src_a[...], dense_ref[:half, :], dims, preferred_element_type=jnp.float32)
            res += lax.dot_general(src_b[...], dense_ref[half:, :], dims, preferred_element_type=jnp.float32)
            out_a[...] = res
        else:
            src = src_a[...]
            out_a[...] = jnp.dot(dense_ref[:half, :], src, preferred_element_type=jnp.float32)
            out_b[...] = jnp.dot(dense_ref[half:, :], src, preferred_element_type=jnp.float32)


def tile_product(tile_block, row_ids, col_ids, live_count, sources, out_tiles, transpose):
    slots = tile_block.shape[0]
    width = sources[0].shape[1]
    steps = slots // CHUNK
    if transpose:
        src_tiles = 2 * sources[0].shape[0] // TILE
        dense_shape = (src_tiles * TILE, out_tiles * TILE)
        out_shapes = [(width, out_tiles * TILE), (8, 128)]
    else:
        sources = (sources[0], jnp.zeros((8, 128), sources[0].dtype))
        src_tiles = sources[0].shape[0] // TILE
        dense_shape = (out_tiles * TILE, src_tiles * TILE)
        out_shapes = [(out_tiles * TILE // 2, width)] * 2

    def tiles_map(i, rows, cols, count):
        last = jnp.maximum(count[0] - 1, 0) // CHUNK
        return (jnp.minimum(i, last), 0, 0)

    def whole(shape):
        return pl.BlockSpec(shape, lambda i, rows, cols, count: (0, 0))

    grid_spec = pltpu.PrefetchScalarGridSpec(
        num_scalar_prefetch=3,
        grid=(steps,),
        in_specs=[pl.BlockSpec((CHUNK, TILE, TILE), tiles_map)] + [whole(x.shape) for x in sources],
        out_specs=[whole(shape) for shape in out_shapes],
        scratch_shapes=[pltpu.VMEM(dense_shape, jnp.bfloat16)],
    )
    first, second = pl.pallas_call(
        lambda *refs: _dense_kernel(transpose, *refs),
        grid_spec=grid_spec,
        out_shape=[jax.ShapeDtypeStruct(shape, jnp.float32) for shape in out_shapes],
        compiler_params=pltpu.CompilerParams(dimension_semantics=("arbitrary",)),
    )(row_ids, col_ids, live_count.reshape(1), tile_block, *sources)
    if transpose:
        return first.T
    return first, second


def gather_rows(x, axis):
    n = lax.psum(1, axis)
    spread = jnp.broadcast_to(x[None], (n,) + x.shape)
    got = lax.all_to_all(spread, axis, 0, 0, tiled=False)
    return got.reshape(n * x.shape[0], x.shape[1])


def scatter_rows(x, axis):
    n = lax.psum(1, axis)
    got = lax.all_to_all(x.reshape(n, -1, x.shape[1]), axis, 0, 0, tiled=False)
    return jnp.sum(got, axis=0)


def swap_core(x, axis="core"):
    return lax.ppermute(x, axis, [(0, 1), (1, 0)])


def ring_gather(x, axis):
    n = lax.psum(1, axis)
    me = lax.axis_index(axis)
    parts = [x] + [lax.ppermute(x, axis, [(i, (i + k) % n) for i in range(n)]) for k in range(1, n)]
    stacked = jnp.stack(parts[::-1])
    return jnp.roll(stacked, me + 1, axis=0).reshape(n * x.shape[0], x.shape[1])


def ring_scatter(x, axis):
    n = lax.psum(1, axis)
    me = lax.axis_index(axis)
    size = x.shape[0] // n
    total = lax.dynamic_slice_in_dim(x, me * size, size, 0)
    for k in range(1, n):
        piece = lax.dynamic_slice_in_dim(x, ((me + k) % n) * size, size, 0)
        total = total + lax.ppermute(piece, axis, [(i, (i + k) % n) for i in range(n)])
    return total


def pair_scatter(x, axis):
    half = x.shape[0] // 2
    me = lax.axis_index(axis)
    mine = lax.dynamic_slice_in_dim(x, me * half, half, 0)
    other = lax.dynamic_slice_in_dim(x, (1 - me) * half, half, 0)
    return mine + swap_core(other, axis)


def pair_gather(x, axis):
    other = swap_core(x, axis)
    first = lax.axis_index(axis) == 0
    return jnp.where(first, jnp.concatenate([x, other]), jnp.concatenate([other, x]))


def reduce_all(x, axes):
    summed = pair_scatter(x, "core")
    summed = gather_rows(scatter_rows(summed, axes), axes)
    return pair_gather(summed, "core")


def head_block(agg, bias, w_out, node_labels):
    pre_act = agg + bias[None, :]
    squash = jax.nn.sigmoid(pre_act)
    hidden = (pre_act * squash).astype(jnp.bfloat16)
    logits = jnp.dot(hidden, w_out, preferred_element_type=jnp.float32)
    top_val = jnp.max(logits, axis=1)
    lse = top_val + jnp.log(jnp.sum(jnp.exp(logits - top_val[:, None]), axis=1))
    onehot = (jnp.arange(w_out.shape[1], dtype=jnp.int32)[None, :] == node_labels[:, None]).astype(
        jnp.float32
    )
    picked = jnp.sum(logits * onehot, axis=1)
    loss_sum = jnp.sum(lse - picked)
    dlog = (jnp.exp(logits - lse[:, None]) - onehot).astype(jnp.bfloat16)
    out_term = jnp.einsum("nf,nc->fc", hidden, dlog, preferred_element_type=jnp.float32)
    d_hidden = jnp.einsum("nc,fc->nf", dlog, w_out, preferred_element_type=jnp.float32)
    grad_z = (d_hidden * squash * (1.0 + pre_act * (1.0 - squash))).astype(jnp.bfloat16)
    bias_term = jnp.sum(grad_z.astype(jnp.float32), axis=0)
    return (loss_sum, out_term, bias_term, grad_z)


def body(features, w_in, bias, w_out, tiles, tile_rows, tile_cols, tile_count, labels):
    row_devices = lax.psum(1, ("y", "zh", "core"))
    col_devices = lax.psum(1, ("cx", "cz"))
    rows_here = features.shape[0]
    feat = features.shape[1]
    classes = w_out.shape[1]
    nodes = rows_here * row_devices * col_devices
    scale = 1.0 / math.sqrt(rows_here)
    row_tiles = row_devices * rows_here // TILE
    col_tiles = col_devices * rows_here // TILE
    tile_block = tiles[0, 0]
    row_ids = tile_rows[0, 0]
    col_ids = tile_cols[0, 0]
    live_count = tile_count[0, 0]
    row_hi = row_ids // 2
    row_pos = jnp.where(row_ids % 2 == lax.axis_index("core"), row_hi, row_hi + row_tiles // 2)
    proj = jnp.dot(features, w_in, preferred_element_type=jnp.float32).astype(jnp.bfloat16)
    source = ring_gather(ring_gather(proj, "cz"), "cx")
    mine, other = tile_product(tile_block, row_pos, col_ids, live_count, (source,), row_tiles, False)
    summed = mine + swap_core(other)
    agg = pair_scatter(ring_scatter(summed, "y"), "zh")
    loss_sum, out_term, bias_term, grad_z = head_block(agg, bias, w_out, labels)
    gathered = ring_gather(ring_gather(grad_z, "zh"), "y")
    sources = (gathered, swap_core(gathered))
    back_part = tile_product(tile_block, row_pos, col_ids, live_count, sources, col_tiles, True)
    grad_proj = ring_scatter(ring_scatter(back_part, "cx"), "cz").astype(jnp.bfloat16)
    in_term = jnp.einsum("nf,ng->fg", features, grad_proj, preferred_element_type=jnp.float32)
    extra = jnp.zeros((feat, 2), jnp.float32)
    extra = extra.at[:, 0].set(bias_term).at[0, 1].set(loss_sum)
    packed = jnp.concatenate([in_term, out_term, extra], axis=1)
    packed = reduce_all(packed, ("y", "zh", "cx", "cz"))
    grad_w_in = packed[:, :feat] * scale
    grad_w_out = packed[:, feat : feat + classes] * scale
    grad_bias = packed[:, feat + classes] * scale
    loss = packed[0, feat + classes + 1] / nodes
    grad_x = jnp.einsum("ng,fg->nf", grad_proj, w_in, preferred_element_type=jnp.float32).astype(
        jnp.bfloat16
    )
    return (loss, grad_x, grad_w_in, grad_w_out, grad_bias)


def solution(mesh):
    row_size, col_size = mesh.shape["row"], mesh.shape["col"]
    cz = 4 if col_size % 4 == 0 else 1
    fine = Mesh(
        mesh.devices.reshape(row_size // 4, 2, 2, col_size // cz, cz),
        ("y", "zh", "core", "cx", "cz"),
    )
    row, col = ("y", "zh", "core"), ("cx", "cz")
    placed = (
        P(row + col, None),
        P(),
        P(),
        P(),
        P(row, col, None, None, None),
        P(row, col, None),
        P(row, col, None),
        P(row, col),
        P(col + row),
    )
    return jax.shard_map(
        body,
        mesh=fine,
        in_specs=placed,
        out_specs=(P(), P(row + col, None), P(), P(), P()),
        check_vma=False,
    )
```
